256 devices in a mesh: blk: 64 (over z, x, core), lane: 4 (over y).
Axes of the slice: x: 4, y: 4, z: 8, core: 2. Of those that a mesh axis runs over, the one named last changes fastest.
Arguments:
- tangent_blocks: bfloat16 [8192, 64, 512], P('blk', None, 'lane'), may hold values from -0.75 to 0.75
- tangent_columns: int32 [8192, 8], P('blk', 'lane'), may hold values from 0 to 8191, as said below
- prolong_blocks: bfloat16 [8192, 24, 512], P('blk'), may hold values from -0.375 to 0.375
- prolong_columns: int32 [8192, 8], P('blk'), may hold values from 0 to 255, as said below
Outputs:
- coarse_band: float32 [256, 24, 672], P(('blk', 'lane'))
The draws below stay inside these ranges and needn't reach their ends.
Inputs may be any that keep to these rules, and one draw needn't show every extreme that they name: tangent_columns[i, 0] = i; every entry of row i is a fine block row of the slab i // 128 or one of the 32 rows on either side of that slab, counted cyclically over the 8192 rows. The 8 entries of a row are distinct; prolong_columns[i, 0] = (i // 128) * 4 + ((i mod 128) * 4) // 128; every entry c of row i has c // 4 equal to i // 128, one more or one less, cyclically over 64 slabs.
All inputs are finite; a program needn't handle non-finite values.
Results may differ from the reference program's by a relative error of at most 0.0029.
Values may be sent and summed in bfloat16 or wider, within the bound.
No kernel may reach another device: no remote copies, remote signals or barrier semaphores. Data moves between devices by JAX's collectives and lax.ppermute only.
A program may use at most 128 MiB of HBM per device.

```python
import jax
import jax.numpy as jnp
from jax import lax

B = 64
CB = 24
KA = 8
KP = 8
NCD = 4
BR = 128
HB = 32
NF = 8192
NC = 256


def draw_tangent_columns(key, part):
    row_ids = jnp.arange(NF, dtype=jnp.int32)
    offsets = jax.random.randint(key, (NF, KA), 0, BR + 2 * HB, dtype=jnp.int32)
    shifted = (row_ids // BR * BR - HB)[:, None] + offsets
    columns = jnp.mod(shifted, NF)
    leading = jnp.arange(KA, dtype=jnp.int32)[None, :] == 0
    return jnp.where(leading, row_ids[:, None], columns).astype(jnp.int32)


def draw_prolong_columns(key, part):
    row_ids = jnp.arange(NF, dtype=jnp.int32)
    slab_ids = row_ids // BR
    own_slot = NCD + row_ids % BR * NCD // BR
    candidates = jnp.arange(3 * NCD, dtype=jnp.int32)
    scores = jax.random.randint(key, (NF, 3 * NCD), 0, 1 << 20, dtype=jnp.int32) * (3 * NCD) + candidates[None, :]
    scores = jnp.where(candidates[None, :] == own_slot[:, None], -1, scores)
    chosen = jnp.argsort(scores, axis=1)[:, :KP].astype(jnp.int32)
    slab_count = NF // BR
    result = jnp.mod(slab_ids[:, None] - 1 + chosen // NCD, slab_count) * NCD + chosen % NCD
    return result.astype(jnp.int32)


def block_scale(rng, shape, shards, least, top_value):
    def one(dim, parts):
        draws = jax.random.uniform(jax.random.fold_in(jax.random.fold_in(rng, 6), dim), (parts,), jnp.float32, least / len(shards), top_value / len(shards))
        return jnp.repeat(jnp.exp(draws), shape[dim] // parts).reshape((-1,) + (1,) * (len(shape) - dim - 1))

    loudness = one(*shards[0])
    for cut in shards[1:]:
        loudness = loudness * one(*cut)
    return loudness


def centred(key, extent, deviation, bound, cuts=(), held_as=jnp.bfloat16):
    gain = block_scale(key, extent, cuts, -0.22, 0.18) if cuts else 1.0
    values = jax.random.normal(key, extent, jnp.float32) * deviation * gain
    return jnp.minimum(jnp.maximum(values, -bound), bound).astype(held_as)


def setup_inputs(seed: int = 0) -> dict:
    streams_of = jax.random.split(jax.random.key(seed), 5)
    return {
        "tangent_blocks": centred(streams_of[0], (NF, B, KA * B), B ** -0.5, 0.75, ((0, 64), (2, 4))),
        "tangent_columns": draw_tangent_columns(jax.random.fold_in(streams_of[4], 71), 0),
        "prolong_blocks": centred(streams_of[2], (NF, CB, KP * B), (4 * B) ** -0.5, 0.375, ((0, 64),)),
        "prolong_columns": draw_prolong_columns(jax.random.fold_in(streams_of[4], 71), 0),
    }


def window_rows(block_values, block_columns, slab_index, slab_count):
    row_count = block_values.shape[0]
    positions = ((block_columns // NCD - slab_index + 2) % slab_count) * NCD + block_columns % NCD
    onehot = (positions[:, :, None] == jnp.arange(5 * NCD, dtype=jnp.int32)[None, None, :]).astype(jnp.float32)
    pieces = block_values.astype(jnp.float32).reshape(row_count, CB, KP, B)
    placed = jnp.einsum("rapx,rpw->rxwa", pieces, onehot)
    return placed.reshape(row_count, B, 5 * NCD * CB).astype(jnp.bfloat16)


def reference(tangent_blocks, tangent_columns, prolong_blocks, prolong_columns):
    slab_count = NF // BR
    halo_rows = BR // 4
    coarse_width = NCD * CB

    def slab_terms(slab_index):
        start = (slab_index * BR).astype(jnp.int32)
        near_rows = ((start - halo_rows + jnp.arange(BR + 2 * halo_rows, dtype=jnp.int32)) % NF).astype(jnp.int32)
        column_side = window_rows(prolong_blocks[near_rows], prolong_columns[near_rows], slab_index, slab_count)
        row_side = column_side[halo_rows:halo_rows + BR, :, coarse_width:4 * coarse_width]
        flat_side = row_side.reshape(BR * B, 3 * coarse_width)
        local_blocks = lax.dynamic_slice_in_dim(tangent_blocks, start, BR, 0)
        local_columns = lax.dynamic_slice_in_dim(tangent_columns, start, BR, 0)
        positions = ((local_columns - start + halo_rows) % NF).astype(jnp.int32)
        result = jnp.zeros((3 * coarse_width, 5 * coarse_width), jnp.float32)
        for neighbour in range(KA):
            picked = column_side[positions[:, neighbour]]
            matrix_block = local_blocks[:, :, neighbour * B:(neighbour + 1) * B]
            product = jnp.einsum("ixy,iyc->ixc", matrix_block.astype(jnp.float32), picked.astype(jnp.float32))
            product = product.astype(jnp.bfloat16)
            result = result + jnp.dot(flat_side.T, product.reshape(BR * B, 5 * coarse_width), preferred_element_type=jnp.float32)
        return result.reshape(3, NCD, CB, 5 * coarse_width)

    gathered = lax.map(slab_terms, jnp.arange(slab_count, dtype=jnp.int32))
    lead = ((0, 0), (0, 0), (0, 0))
    own_part = jnp.pad(gathered[:, 1], lead + ((coarse_width, coarse_width),))
    from_lower = jnp.pad(jnp.roll(gathered[:, 2], 1, axis=0), lead + ((0, 2 * coarse_width),))
    from_upper = jnp.pad(jnp.roll(gathered[:, 0], -1, axis=0), lead + ((2 * coarse_width, 0),))
    return (own_part + from_lower + from_upper).reshape(NC, CB, 7 * coarse_width)
```

```python
import functools

import jax
import jax.numpy as jnp
from jax import lax
from jax.experimental import pallas as pl
from jax.experimental.pallas import tpu as pltpu
from jax.sharding import PartitionSpec as P

B = 64
CB = 24
KP = 8
NCD = 4
GROUP = 8


def shifted(value, axis, steps):
    count = lax.axis_size(axis)
    pairs = [(source, (source + steps) % count) for source in range(count)]
    return lax.ppermute(value, axis, pairs)


def widen(values, left_pad, right_pad):
    return jnp.pad(values, ((0, 0),) * (values.ndim - 1) + ((left_pad, right_pad),))


def slab_kernel(halo_rows, row_count, local_k, wpos_ref, jloc_ref, pb_ref, tb_ref, gt_ref,
                s_ref, xs_ref, w_ref):
    window_slots = 5 * NCD
    row_slots = 3 * NCD
    f32 = jnp.float32
    bf16 = jnp.bfloat16
    upper24 = lax.broadcasted_iota(jnp.int32, (CB, 128), 1) >= B
    upper64 = lax.broadcasted_iota(jnp.int32, (B, 128), 1) >= B
    gt_ref[...] = jnp.zeros(gt_ref.shape, f32)
    w_ref[...] = jnp.zeros(w_ref.shape, bf16)

    def place(dst, slot, lane_group, upper, r, p):
        src = pb_ref[r, :, (p // 2) * 128:(p // 2) * 128 + 128].astype(f32)
        if (p % 2 == 1) != upper:
            src = pltpu.roll(src, B, 1)
        keep = upper24 if upper else jnp.logical_not(upper24)
        rows = pl.ds(pl.multiple_of(slot * CB, 8), CB)
        lanes = slice(lane_group * 128, lane_group * 128 + 128)
        dst[rows, lanes] = dst[rows, lanes] + jnp.where(keep, src, 0.0)

    def group(g, carry):
        base = g * GROUP
        xs_ref[...] = jnp.zeros(xs_ref.shape, f32)
        for m in range(GROUP):
            r = base + m + halo_rows
            for p in range(KP):
                w = wpos_ref[r * KP + p]
                slot = jnp.clip(w - NCD, 0, row_slots - 1)
                place(xs_ref, slot, m // 2, m % 2 == 1, r, p)
        xsb = xs_ref[...].astype(bf16)
        for k in range(local_k):
            s_ref[...] = jnp.zeros(s_ref.shape, f32)
            for m in range(GROUP):
                r = jloc_ref[(base + m) * local_k + k]
                for p in range(KP):
                    w = wpos_ref[r * KP + p]
                    slot = jnp.clip(w, 0, window_slots - 1)
                    place(s_ref, slot, m // 2, m % 2 == 1, r, p)
            parts = []
            for c in range(GROUP // 4):
                for mm in range(4):
                    t = tb_ref[base + 4 * c + mm].astype(f32)
                    if (k % 2 == 1) != (mm % 2 == 1):
                        t = pltpu.roll(t, B, 1)
                    keep = upper64 if mm % 2 == 1 else jnp.logical_not(upper64)
                    w_ref[mm * B:(mm + 1) * B, (mm // 2) * 128:(mm // 2) * 128 + 128] = jnp.where(
                        keep, t, 0.0
                    ).astype(bf16)
                window = s_ref[:, c * 256:(c + 1) * 256].astype(bf16)
                q = lax.dot_general(
                    window, w_ref[...], (((1,), (1,)), ((), ())), preferred_element_type=f32
                )
                parts.append(q.astype(bf16))
            qt = jnp.concatenate(parts, axis=1)
            gt_ref[...] += lax.dot_general(
                qt, xsb, (((1,), (1,)), ((), ())), preferred_element_type=f32
            )
        return carry

    lax.fori_loop(0, row_count // GROUP, group, 0)


def slab_terms_t(wpos, jloc, pb, tb, halo_rows, row_count):
    local_k = tb.shape[2] // B
    window_width = 5 * NCD * CB
    row_width = 3 * NCD * CB
    kernel = functools.partial(slab_kernel, halo_rows, row_count, local_k)
    flops = 2 * row_count * local_k * (window_width * 256 * B + window_width * row_width * B)
    return pl.pallas_call(
        kernel,
        out_shape=jax.ShapeDtypeStruct((window_width, row_width), jnp.float32),
        in_specs=[
            pl.BlockSpec(memory_space=pltpu.SMEM),
            pl.BlockSpec(memory_space=pltpu.SMEM),
            pl.BlockSpec(memory_space=pltpu.VMEM),
            pl.BlockSpec(memory_space=pltpu.VMEM),
        ],
        out_specs=pl.BlockSpec(memory_space=pltpu.VMEM),
        scratch_shapes=[
            pltpu.VMEM((window_width, GROUP * B), jnp.float32),
            pltpu.VMEM((row_width, GROUP * B), jnp.float32),
            pltpu.VMEM((256, 256), jnp.bfloat16),
        ],
        compiler_params=pltpu.CompilerParams(vmem_limit_bytes=48 * 1024 * 1024),
        cost_estimate=pl.CostEstimate(
            flops=flops,
            bytes_accessed=pb.size * 2 + tb.size * 2 + window_width * row_width * 4,
            transcendentals=0,
        ),
    )(wpos, jloc, pb, tb)


def on_device(tangent_blocks, tangent_columns, prolong_blocks, prolong_columns):
    slab_count = lax.axis_size("blk")
    slab_index = lax.axis_index("blk")
    lane_count = lax.axis_size("lane")
    lane_index = lax.axis_index("lane")
    row_count = prolong_blocks.shape[0]
    halo_rows = row_count // 4
    coarse_width = NCD * CB
    fine_count = row_count * slab_count

    lower_blocks = shifted(prolong_blocks[row_count - halo_rows:], "blk", 1)
    upper_blocks = shifted(prolong_blocks[:halo_rows], "blk", -1)
    lower_columns = shifted(prolong_columns[row_count - halo_rows:], "blk", 1)
    upper_columns = shifted(prolong_columns[:halo_rows], "blk", -1)
    near_blocks = jnp.concatenate([lower_blocks, prolong_blocks, upper_blocks], axis=0)
    near_columns = jnp.concatenate([lower_columns, prolong_columns, upper_columns], axis=0)
    wpos = ((near_columns // NCD - slab_index + 2) % slab_count) * NCD + near_columns % NCD
    wpos = wpos.astype(jnp.int32).reshape(-1)
    jloc = (tangent_columns - slab_index * row_count + halo_rows) % fine_count
    jloc = jnp.clip(jloc, 0, row_count + 2 * halo_rows - 1).astype(jnp.int32).reshape(-1)

    gt = slab_terms_t(wpos, jloc, near_blocks, tangent_blocks, halo_rows, row_count)
    terms = gt.T.reshape(3, NCD, CB, 5 * coarse_width)

    shares = lax.dynamic_index_in_dim(terms, lane_index, axis=1, keepdims=False)
    for step in range(1, lane_count):
        piece = lax.dynamic_index_in_dim(
            terms, (lane_index + step) % lane_count, axis=1, keepdims=False
        )
        shares = shares + shifted(piece, "lane", step)
    from_lower = shifted(shares[2], "blk", 1)
    from_upper = shifted(shares[0], "blk", -1)
    coarse_band = (
        widen(shares[1], coarse_width, coarse_width)
        + widen(from_lower, 0, 2 * coarse_width)
        + widen(from_upper, 2 * coarse_width, 0)
    )
    return coarse_band[None]


def solution(mesh):
    return jax.shard_map(
        on_device,
        mesh=mesh,
        in_specs=(P("blk", None, "lane"), P("blk", "lane"), P("blk", None, None), P("blk", None)),
        out_specs=P(("blk", "lane"), None, None),
        check_vma=False,
    )
```

```python
import functools

import jax
import jax.numpy as jnp
from jax import lax
from jax.experimental import pallas as pl
from jax.experimental.pallas import tpu as pltpu
from jax.sharding import PartitionSpec as P

B = 64
CB = 24
KP = 8
NCD = 4
GROUP = 8


def shifted(value, axis, steps):
    count = lax.axis_size(axis)
    pairs = [(source, (source + steps) % count) for source in range(count)]
    return lax.ppermute(value, axis, pairs)


def widen(values, left_pad, right_pad):
    return jnp.pad(values, ((0, 0),) * (values.ndim - 1) + ((left_pad, right_pad),))


def slab_kernel(halo_rows, row_count, local_k, wpos_ref, jloc_ref, pb_ref, tb_ref, gt_ref,
                s_ref, xs_ref, w_ref):
    window_slots = 5 * NCD
    row_slots = 3 * NCD
    f32 = jnp.float32
    bf16 = jnp.bfloat16
    upper24 = lax.broadcasted_iota(jnp.int32, (CB, 128), 1) >= B
    upper64 = lax.broadcasted_iota(jnp.int32, (B, 128), 1) >= B
    gt_ref[...] = jnp.zeros(gt_ref.shape, f32)
    w_ref[...] = jnp.zeros(w_ref.shape, bf16)

    def place(dst, slot, lane_group, upper, r, p):
        src = pb_ref[r, :, (p // 2) * 128:(p // 2) * 128 + 128].astype(f32)
        if (p % 2 == 1) != upper:
            src = pltpu.roll(src, B, 1)
        keep = upper24 if upper else jnp.logical_not(upper24)
        rows = pl.ds(pl.multiple_of(slot * CB, 8), CB)
        lanes = slice(lane_group * 128, lane_group * 128 + 128)
        dst[rows, lanes] = dst[rows, lanes] + jnp.where(keep, src, 0.0)

    def group(g, carry):
        base = g * GROUP
        xs_ref[...] = jnp.zeros(xs_ref.shape, f32)
        for m in range(GROUP):
            r = base + m + halo_rows
            for p in range(KP):
                w = wpos_ref[r * KP + p]
                slot = jnp.clip(w - NCD, 0, row_slots - 1)
                place(xs_ref, slot, m // 2, m % 2 == 1, r, p)
        xsb = xs_ref[...].astype(bf16)
        for k in range(local_k):
            s_ref[...] = jnp.zeros(s_ref.shape, f32)
            for m in range(GROUP):
                r = jloc_ref[(base + m) * local_k + k]
                for p in range(KP):
                    w = wpos_ref[r * KP + p]
                    slot = jnp.clip(w, 0, window_slots - 1)
                    place(s_ref, slot, m // 2, m % 2 == 1, r, p)
            parts = []
            for c in range(GROUP // 4):
                for mm in range(4):
                    t = tb_ref[base + 4 * c + mm].astype(f32)
                    if (k % 2 == 1) != (mm % 2 == 1):
                        t = pltpu.roll(t, B, 1)
                    keep = upper64 if mm % 2 == 1 else jnp.logical_not(upper64)
                    w_ref[mm * B:(mm + 1) * B, (mm // 2) * 128:(mm // 2) * 128 + 128] = jnp.where(
                        keep, t, 0.0
                    ).astype(bf16)
                window = s_ref[:, c * 256:(c + 1) * 256].astype(bf16)
                q = lax.dot_general(
                    window, w_ref[...], (((1,), (1,)), ((), ())), preferred_element_type=f32
                )
                parts.append(q.astype(bf16))
            qt = jnp.concatenate(parts, axis=1)
            gt_ref[...] += lax.dot_general(
                qt, xsb, (((1,), (1,)), ((), ())), preferred_element_type=f32
            )
        return carry

    lax.fori_loop(0, row_count // GROUP, group, 0)


def slab_terms_t(wpos, jloc, pb, tb, halo_rows, row_count):
    local_k = tb.shape[2] // B
    window_width = 5 * NCD * CB
    row_width = 3 * NCD * CB
    kernel = functools.partial(slab_kernel, halo_rows, row_count, local_k)
    flops = 2 * row_count * local_k * (window_width * 256 * B + window_width * row_width * B)
    return pl.pallas_call(
        kernel,
        out_shape=jax.ShapeDtypeStruct((window_width, row_width), jnp.float32),
        in_specs=[
            pl.BlockSpec(memory_space=pltpu.SMEM),
            pl.BlockSpec(memory_space=pltpu.SMEM),
            pl.BlockSpec(memory_space=pltpu.VMEM),
            pl.BlockSpec(memory_space=pltpu.VMEM),
        ],
        out_specs=pl.BlockSpec(memory_space=pltpu.VMEM),
        scratch_shapes=[
            pltpu.VMEM((window_width, GROUP * B), jnp.float32),
            pltpu.VMEM((row_width, GROUP * B), jnp.float32),
            pltpu.VMEM((256, 256), jnp.bfloat16),
        ],
        compiler_params=pltpu.CompilerParams(vmem_limit_bytes=48 * 1024 * 1024),
        cost_estimate=pl.CostEstimate(
            flops=flops,
            bytes_accessed=pb.size * 2 + tb.size * 2 + window_width * row_width * 4,
            transcendentals=0,
        ),
    )(wpos, jloc, pb, tb)


def on_device(tangent_blocks, tangent_columns, prolong_blocks, prolong_columns):
    slab_count = lax.axis_size("blk")
    slab_index = lax.axis_index("blk")
    lane_count = lax.axis_size("lane")
    lane_index = lax.axis_index("lane")
    row_count = prolong_blocks.shape[0]
    halo_rows = row_count // 4
    coarse_width = NCD * CB
    fine_count = row_count * slab_count

    lower_blocks = shifted(prolong_blocks[row_count - halo_rows:], "blk", 1)
    upper_blocks = shifted(prolong_blocks[:halo_rows], "blk", -1)
    lower_columns = shifted(prolong_columns[row_count - halo_rows:], "blk", 1)
    upper_columns = shifted(prolong_columns[:halo_rows], "blk", -1)
    near_blocks = jnp.concatenate([lower_blocks, prolong_blocks, upper_blocks], axis=0)
    near_columns = jnp.concatenate([lower_columns, prolong_columns, upper_columns], axis=0)
    wpos = ((near_columns // NCD - slab_index + 2) % slab_count) * NCD + near_columns % NCD
    wpos = wpos.astype(jnp.int32).reshape(-1)
    jloc = (tangent_columns - slab_index * row_count + halo_rows) % fine_count
    jloc = jnp.clip(jloc, 0, row_count + 2 * halo_rows - 1).astype(jnp.int32).reshape(-1)

    gt = slab_terms_t(wpos, jloc, near_blocks, tangent_blocks, halo_rows, row_count)
    terms = gt.T.reshape(3, NCD, CB, 5 * coarse_width)

    combined = ("blk", "lane")
    device_count = slab_count * lane_count
    bands = []
    for slab_step in (1, 0, -1):
        total = None
        for lane_step in range(lane_count):
            piece = lax.dynamic_index_in_dim(
                terms[1 + slab_step], (lane_index + lane_step) % lane_count, axis=0, keepdims=False
            )
            if slab_step != 0 or lane_step != 0:
                pairs = []
                for source in range(device_count):
                    s_src, l_src = divmod(source, lane_count)
                    target = ((s_src + slab_step) % slab_count) * lane_count + (l_src + lane_step) % lane_count
                    pairs.append((source, target))
                piece = lax.ppermute(piece, combined, pairs)
            total = piece if total is None else total + piece
        bands.append(total)
    from_lower, own, from_upper = bands
    coarse_band = (
        widen(own, coarse_width, coarse_width)
        + widen(from_lower, 0, 2 * coarse_width)
        + widen(from_upper, 2 * coarse_width, 0)
    )
    return coarse_band[None]


def solution(mesh):
    return jax.shard_map(
        on_device,
        mesh=mesh,
        in_specs=(P("blk", None, "lane"), P("blk", "lane"), P("blk", None, None), P("blk", None)),
        out_specs=P(("blk", "lane"), None, None),
        check_vma=False,
    )
```

```python
import functools

import jax
import jax.numpy as jnp
from jax import lax
from jax.experimental import pallas as pl
from jax.experimental.pallas import tpu as pltpu
from jax.sharding import PartitionSpec as P

B = 64
CB = 24
KP = 8
NCD = 4
GROUP = 8


def shifted(value, axis, steps):
    count = lax.axis_size(axis)
    pairs = [(source, (source + steps) % count) for source in range(count)]
    return lax.ppermute(value, axis, pairs)


def widen(values, left_pad, right_pad):
    return jnp.pad(values, ((0, 0),) * (values.ndim - 1) + ((left_pad, right_pad),))


def slab_kernel(halo_rows, row_count, local_k, wpos_ref, jloc_ref, pb_ref, tb_ref, gt_ref,
                s_ref, xs_ref, w_ref):
    window_slots = 5 * NCD
    row_slots = 3 * NCD
    f32 = jnp.float32
    bf16 = jnp.bfloat16
    upper24 = lax.broadcasted_iota(jnp.int32, (CB, 128), 1) >= B
    upper64 = lax.broadcasted_iota(jnp.int32, (B, 128), 1) >= B
    gt_ref[...] = jnp.zeros(gt_ref.shape, f32)
    w_ref[...] = jnp.zeros(w_ref.shape, bf16)

    def place(dst, slot, lane_group, upper, r, p):
        src = pb_ref[r, :, (p // 2) * 128:(p // 2) * 128 + 128].astype(f32)
        if (p % 2 == 1) != upper:
            src = pltpu.roll(src, B, 1)
        keep = upper24 if upper else jnp.logical_not(upper24)
        rows = pl.ds(pl.multiple_of(slot * CB, 8), CB)
        lanes = slice(lane_group * 128, lane_group * 128 + 128)
        dst[rows, lanes] = dst[rows, lanes] + jnp.where(keep, src, 0.0)

    def group(g, carry):
        base = g * GROUP
        xs_ref[...] = jnp.zeros(xs_ref.shape, f32)
        for m in range(GROUP):
            r = base + m + halo_rows
            for p in range(KP):
                w = wpos_ref[r * KP + p]
                slot = jnp.clip(w - NCD, 0, row_slots - 1)
                place(xs_ref, slot, m // 2, m % 2 == 1, r, p)
        xsb = xs_ref[...].astype(bf16)
        for k in range(local_k):
            s_ref[...] = jnp.zeros(s_ref.shape, f32)
            for m in range(GROUP):
                r = jloc_ref[(base + m) * local_k + k]
                for p in range(KP):
                    w = wpos_ref[r * KP + p]
                    slot = jnp.clip(w, 0, window_slots - 1)
                    place(s_ref, slot, m // 2, m % 2 == 1, r, p)
            parts = []
            for c in range(GROUP // 4):
                for mm in range(4):
                    t = tb_ref[base + 4 * c + mm].astype(f32)
                    if (k % 2 == 1) != (mm % 2 == 1):
                        t = pltpu.roll(t, B, 1)
                    keep = upper64 if mm % 2 == 1 else jnp.logical_not(upper64)
                    w_ref[mm * B:(mm + 1) * B, (mm // 2) * 128:(mm // 2) * 128 + 128] = jnp.where(
                        keep, t, 0.0
                    ).astype(bf16)
                window = s_ref[:, c * 256:(c + 1) * 256].astype(bf16)
                q = lax.dot_general(
                    window, w_ref[...], (((1,), (1,)), ((), ())), preferred_element_type=f32
                )
                parts.append(q.astype(bf16))
            qt = jnp.concatenate(parts, axis=1)
            gt_ref[...] += lax.dot_general(
                qt, xsb, (((1,), (1,)), ((), ())), preferred_element_type=f32
            )
        return carry

    lax.fori_loop(0, row_count // GROUP, group, 0)


def slab_terms_t(wpos, jloc, pb, tb, halo_rows, row_count):
    local_k = tb.shape[2] // B
    window_width = 5 * NCD * CB
    row_width = 3 * NCD * CB
    kernel = functools.partial(slab_kernel, halo_rows, row_count, local_k)
    flops = 2 * row_count * local_k * (window_width * 256 * B + window_width * row_width * B)
    return pl.pallas_call(
        kernel,
        out_shape=jax.ShapeDtypeStruct((window_width, row_width), jnp.float32),
        in_specs=[
            pl.BlockSpec(memory_space=pltpu.SMEM),
            pl.BlockSpec(memory_space=pltpu.SMEM),
            pl.BlockSpec(memory_space=pltpu.VMEM),
            pl.BlockSpec(memory_space=pltpu.VMEM),
        ],
        out_specs=pl.BlockSpec(memory_space=pltpu.VMEM),
        scratch_shapes=[
            pltpu.VMEM((window_width, GROUP * B), jnp.float32),
            pltpu.VMEM((row_width, GROUP * B), jnp.float32),
            pltpu.VMEM((256, 256), jnp.bfloat16),
        ],
        compiler_params=pltpu.CompilerParams(vmem_limit_bytes=48 * 1024 * 1024),
        cost_estimate=pl.CostEstimate(
            flops=flops,
            bytes_accessed=pb.size * 2 + tb.size * 2 + window_width * row_width * 4,
            transcendentals=0,
        ),
    )(wpos, jloc, pb, tb)


def on_device(tangent_blocks, tangent_columns, prolong_blocks, prolong_columns):
    slab_count = lax.axis_size("blk")
    slab_index = lax.axis_index("blk")
    lane_count = lax.axis_size("lane")
    lane_index = lax.axis_index("lane")
    row_count = prolong_blocks.shape[0]
    halo_rows = row_count // 4
    coarse_width = NCD * CB
    fine_count = row_count * slab_count

    def with_columns(rows):
        blocks = prolong_blocks[rows]
        columns = prolong_columns[rows].astype(jnp.bfloat16)
        columns = jnp.pad(columns, ((0, 0), (0, blocks.shape[2] - KP)))[:, None, :]
        return jnp.concatenate([blocks, columns], axis=1)

    lower = shifted(with_columns(slice(row_count - halo_rows, row_count)), "blk", 1)
    upper = shifted(with_columns(slice(0, halo_rows)), "blk", -1)
    near_blocks = jnp.concatenate([lower[:, :CB], prolong_blocks, upper[:, :CB]], axis=0)
    near_columns = jnp.concatenate(
        [
            lower[:, CB, :KP].astype(jnp.int32),
            prolong_columns,
            upper[:, CB, :KP].astype(jnp.int32),
        ],
        axis=0,
    )
    wpos = ((near_columns // NCD - slab_index + 2) % slab_count) * NCD + near_columns % NCD
    wpos = wpos.astype(jnp.int32).reshape(-1)
    jloc = (tangent_columns - slab_index * row_count + halo_rows) % fine_count
    jloc = jnp.clip(jloc, 0, row_count + 2 * halo_rows - 1).astype(jnp.int32).reshape(-1)

    gt = slab_terms_t(wpos, jloc, near_blocks, tangent_blocks, halo_rows, row_count)
    terms = gt.T.reshape(3, NCD, CB, 5 * coarse_width)

    shares = lax.dynamic_index_in_dim(terms, lane_index, axis=1, keepdims=False)
    for step in range(1, lane_count):
        piece = lax.dynamic_index_in_dim(
            terms, (lane_index + step) % lane_count, axis=1, keepdims=False
        )
        shares = shares + shifted(piece, "lane", step)
    from_lower = shifted(shares[2], "blk", 1)
    from_upper = shifted(shares[0], "blk", -1)
    coarse_band = (
        widen(shares[1], coarse_width, coarse_width)
        + widen(from_lower, 0, 2 * coarse_width)
        + widen(from_upper, 2 * coarse_width, 0)
    )
    return coarse_band[None]


def solution(mesh):
    return jax.shard_map(
        on_device,
        mesh=mesh,
        in_specs=(P("blk", None, "lane"), P("blk", "lane"), P("blk", None, None), P("blk", None)),
        out_specs=P(("blk", "lane"), None, None),
        check_vma=False,
    )
```

```python
import functools

import jax
import jax.numpy as jnp
from jax import lax
from jax.experimental import pallas as pl
from jax.experimental.pallas import tpu as pltpu
from jax.sharding import PartitionSpec as P

B = 64
CB = 24
KP = 8
NCD = 4
GROUP = 8


def shifted(value, axis, steps):
    count = lax.axis_size(axis)
    pairs = [(source, (source + steps) % count) for source in range(count)]
    return lax.ppermute(value, axis, pairs)


def widen(values, left_pad, right_pad):
    return jnp.pad(values, ((0, 0),) * (values.ndim - 1) + ((left_pad, right_pad),))


NT = (((1,), (1,)), ((), ()))


def half_masks():
    upper24 = lax.broadcasted_iota(jnp.int32, (CB, 128), 1) >= B
    upper64 = lax.broadcasted_iota(jnp.int32, (B, 128), 1) >= B
    return upper24, upper64


def place(src_ref, r, p, dst, slot, lane_group, upper, upper24):
    src = src_ref[r, 0:CB, (p // 2) * 128:(p // 2) * 128 + 128].astype(jnp.float32)
    if (p % 2 == 1) != upper:
        src = pltpu.roll(src, B, 1)
    keep = upper24 if upper else jnp.logical_not(upper24)
    rows = pl.ds(pl.multiple_of(slot * CB, 8), CB)
    lanes = slice(lane_group * 128, lane_group * 128 + 128)
    dst[rows, lanes] = dst[rows, lanes] + jnp.where(keep, src, 0.0)


def place_row_side(pb_ref, wpos_ref, wbase, i, xs_ref, m, upper24):
    for p in range(KP):
        slot = jnp.clip(wpos_ref[wbase + p] - NCD, 0, 3 * NCD - 1)
        place(pb_ref, i, p, xs_ref, slot, m // 2, m % 2 == 1, upper24)


def place_window(src_ref, r, wpos_ref, wbase, s_ref, m, upper24):
    for p in range(KP):
        slot = jnp.clip(wpos_ref[wbase + p], 0, 5 * NCD - 1)
        place(src_ref, r, p, s_ref, slot, m // 2, m % 2 == 1, upper24)


def chunk_product(s_ref, w_ref, c):
    window = s_ref[:, c * 256:(c + 1) * 256].astype(jnp.bfloat16)
    q = lax.dot_general(window, w_ref[...], NT, preferred_element_type=jnp.float32)
    return q.astype(jnp.bfloat16)


def own_kernel(halo_rows, local_k, wpos_ref, jloc_ref, pb_ref, tb_ref, gt_ref, s_ref, xs_ref, w_ref):
    row_count = pb_ref.shape[0]
    f32 = jnp.float32
    upper24, upper64 = half_masks()
    gt_ref[...] = jnp.zeros(gt_ref.shape, f32)
    w_ref[...] = jnp.zeros(w_ref.shape, jnp.bfloat16)

    def group(g, carry):
        base = g * GROUP
        xs_ref[...] = jnp.zeros(xs_ref.shape, f32)
        for m in range(GROUP):
            place_row_side(pb_ref, wpos_ref, (base + m) * KP, base + m, xs_ref, m, upper24)
        xsb = xs_ref[...].astype(jnp.bfloat16)
        for k in range(local_k):
            s_ref[...] = jnp.zeros(s_ref.shape, f32)
            for m in range(GROUP):
                r = jloc_ref[(base + m) * local_k + k] - halo_rows
                inside = jnp.logical_and(r >= 0, r < row_count)
                rr = jnp.clip(r, 0, row_count - 1)

                @pl.when(inside)
                def _():
                    place_window(pb_ref, rr, wpos_ref, rr * KP, s_ref, m, upper24)

            parts = []
            for c in range(GROUP // 4):
                for mm in range(4):
                    t = tb_ref[base + 4 * c + mm].astype(f32)
                    if (k % 2 == 1) != (mm % 2 == 1):
                        t = pltpu.roll(t, B, 1)
                    keep = upper64 if mm % 2 == 1 else jnp.logical_not(upper64)
                    w_ref[mm * B:(mm + 1) * B, (mm // 2) * 128:(mm // 2) * 128 + 128] = jnp.where(
                        keep, t, 0.0
                    ).astype(jnp.bfloat16)
                parts.append(chunk_product(s_ref, w_ref, c))
            qt = jnp.concatenate(parts, axis=1)
            gt_ref[...] += lax.dot_general(qt, xsb, NT, preferred_element_type=f32)
        return carry

    lax.fori_loop(0, row_count // GROUP, group, 0)


def halo_kernel(halo_rows, local_k, count_ref, list_ref, wpos_ref, jloc_ref, pb_ref, lo_ref, up_ref,
                tb_ref, ga_ref, gt_ref, s_ref, xs_ref, w_ref):
    row_count = pb_ref.shape[0]
    f32 = jnp.float32
    upper24, upper64 = half_masks()
    gt_ref[...] = ga_ref[...]

    def group(g, carry):
        s_ref[...] = jnp.zeros(s_ref.shape, f32)
        xs_ref[...] = jnp.zeros(xs_ref.shape, f32)
        parts = []
        for c in range(GROUP // 4):
            for mm in range(4):
                m = 4 * c + mm
                pair = list_ref[g * GROUP + m]
                valid = pair >= 0
                pc = jnp.maximum(pair, 0)
                i = pc // local_k
                k = pc % local_k
                r = jloc_ref[pc]
                t = tb_ref[i].astype(f32)
                same = (k % 2) == (mm % 2)
                t = jnp.where(same, t, pltpu.roll(t, B, 1))
                keep = upper64 if mm % 2 == 1 else jnp.logical_not(upper64)
                keep = jnp.logical_and(keep, valid)
                w_ref[mm * B:(mm + 1) * B, (mm // 2) * 128:(mm // 2) * 128 + 128] = jnp.where(
                    keep, t, 0.0
                ).astype(jnp.bfloat16)

                @pl.when(valid)
                def _():
                    place_row_side(pb_ref, wpos_ref, (i + halo_rows) * KP, i, xs_ref, m, upper24)

                    @pl.when(r < halo_rows)
                    def _():
                        rl = jnp.clip(r, 0, halo_rows - 1)
                        place_window(lo_ref, rl, wpos_ref, r * KP, s_ref, m, upper24)

                    @pl.when(r >= halo_rows + row_count)
                    def _():
                        ru = jnp.clip(r - halo_rows - row_count, 0, halo_rows - 1)
                        place_window(up_ref, ru, wpos_ref, r * KP, s_ref, m, upper24)

            parts.append(chunk_product(s_ref, w_ref, c))
        qt = jnp.concatenate(parts, axis=1)
        xsb = xs_ref[...].astype(jnp.bfloat16)
        gt_ref[...] += lax.dot_general(qt, xsb, NT, preferred_element_type=f32)
        return carry

    lax.fori_loop(0, count_ref[0], group, 0)


def scratch():
    return [
        pltpu.VMEM((5 * NCD * CB, GROUP * B), jnp.float32),
        pltpu.VMEM((3 * NCD * CB, GROUP * B), jnp.float32),
        pltpu.VMEM((256, 256), jnp.bfloat16),
    ]


def own_terms(wpos_own, jloc, pb, tb, halo_rows):
    local_k = tb.shape[2] // B
    row_count = pb.shape[0]
    shape = (5 * NCD * CB, 3 * NCD * CB)
    flops = 2 * row_count * local_k * shape[0] * (256 + shape[1]) * B
    smem = pl.BlockSpec(memory_space=pltpu.SMEM)
    vmem = pl.BlockSpec(memory_space=pltpu.VMEM)
    return pl.pallas_call(
        functools.partial(own_kernel, halo_rows, local_k),
        out_shape=jax.ShapeDtypeStruct(shape, jnp.float32),
        in_specs=[smem, smem, vmem, vmem],
        out_specs=vmem,
        scratch_shapes=scratch(),
        compiler_params=pltpu.CompilerParams(vmem_limit_bytes=48 * 1024 * 1024),
        cost_estimate=pl.CostEstimate(
            flops=flops, bytes_accessed=pb.size * 2 + tb.size * 2 + shape[0] * shape[1] * 4,
            transcendentals=0,
        ),
    )(wpos_own, jloc, pb, tb)


def halo_terms(count, pair_list, wpos, jloc, pb, lower, upper, tb, own_part, halo_rows):
    local_k = tb.shape[2] // B
    shape = own_part.shape
    smem = pl.BlockSpec(memory_space=pltpu.SMEM)
    vmem = pl.BlockSpec(memory_space=pltpu.VMEM)
    flops = 2 * pair_list.shape[0] // 2 * shape[0] * (256 + shape[1]) * B
    return pl.pallas_call(
        functools.partial(halo_kernel, halo_rows, local_k),
        out_shape=jax.ShapeDtypeStruct(shape, jnp.float32),
        in_specs=[smem, smem, smem, smem, vmem, vmem, vmem, vmem, vmem],
        out_specs=vmem,
        scratch_shapes=scratch(),
        compiler_params=pltpu.CompilerParams(vmem_limit_bytes=48 * 1024 * 1024),
        cost_estimate=pl.CostEstimate(
            flops=flops, bytes_accessed=pb.size * 2 + tb.size * 2 + shape[0] * shape[1] * 8,
            transcendentals=0,
        ),
    )(count, pair_list, wpos, jloc, pb, lower, upper, tb, own_part)


def on_device(tangent_blocks, tangent_columns, prolong_blocks, prolong_columns):
    slab_count = lax.axis_size("blk")
    slab_index = lax.axis_index("blk")
    lane_count = lax.axis_size("lane")
    lane_index = lax.axis_index("lane")
    row_count = prolong_blocks.shape[0]
    halo_rows = row_count // 4
    coarse_width = NCD * CB
    fine_count = row_count * slab_count

    def with_columns(rows):
        blocks = prolong_blocks[rows]
        columns = prolong_columns[rows].astype(jnp.bfloat16)
        columns = jnp.pad(columns, ((0, 0), (0, blocks.shape[2] - KP)))[:, None, :]
        return jnp.concatenate([blocks, columns], axis=1)

    lower = shifted(with_columns(slice(row_count - halo_rows, row_count)), "blk", 1)
    upper = shifted(with_columns(slice(0, halo_rows)), "blk", -1)

    def window_slots(columns):
        slots = ((columns // NCD - slab_index + 2) % slab_count) * NCD + columns % NCD
        return slots.astype(jnp.int32)

    wpos_own = window_slots(prolong_columns)
    jloc = (tangent_columns - slab_index * row_count + halo_rows) % fine_count
    jloc = jnp.clip(jloc, 0, row_count + 2 * halo_rows - 1).astype(jnp.int32).reshape(-1)

    own_part = own_terms(wpos_own.reshape(-1), jloc, prolong_blocks, tangent_blocks, halo_rows)

    pair_count = jloc.shape[0]
    in_halo = jnp.logical_or(jloc < halo_rows, jloc >= halo_rows + row_count)
    order = jnp.cumsum(in_halo.astype(jnp.int32)) - 1
    slots = jnp.arange(pair_count, dtype=jnp.int32)
    match = jnp.logical_and(in_halo[None, :], order[None, :] == slots[:, None])
    pair_list = jnp.where(
        jnp.any(match, axis=1), jnp.sum(jnp.where(match, slots[None, :], 0), axis=1), -1
    ).astype(jnp.int32)
    halo_count = jnp.sum(in_halo.astype(jnp.int32))
    group_count = ((halo_count + GROUP - 1) // GROUP).astype(jnp.int32).reshape(1)

    lower_columns = lower[:, CB, :KP].astype(jnp.int32)
    upper_columns = upper[:, CB, :KP].astype(jnp.int32)
    wpos = jnp.concatenate(
        [window_slots(lower_columns), wpos_own, window_slots(upper_columns)], axis=0
    ).reshape(-1)
    gt = halo_terms(group_count, pair_list, wpos, jloc, prolong_blocks, lower, upper,
                    tangent_blocks, own_part, halo_rows)
    terms = gt.T.reshape(3, NCD, CB, 5 * coarse_width)

    shares = lax.dynamic_index_in_dim(terms, lane_index, axis=1, keepdims=False)
    for step in range(1, lane_count):
        piece = lax.dynamic_index_in_dim(
            terms, (lane_index + step) % lane_count, axis=1, keepdims=False
        )
        shares = shares + shifted(piece, "lane", step)
    from_lower = shifted(shares[2], "blk", 1)
    from_upper = shifted(shares[0], "blk", -1)
    coarse_band = (
        widen(shares[1], coarse_width, coarse_width)
        + widen(from_lower, 0, 2 * coarse_width)
        + widen(from_upper, 2 * coarse_width, 0)
    )
    return coarse_band[None]


def solution(mesh):
    return jax.shard_map(
        on_device,
        mesh=mesh,
        in_specs=(P("blk", None, "lane"), P("blk", "lane"), P("blk", None, None), P("blk", None)),
        out_specs=P(("blk", "lane"), None, None),
        check_vma=False,
    )
```

```python
import functools

import jax
import jax.numpy as jnp
from jax import lax
from jax.experimental import pallas as pl
from jax.experimental.pallas import tpu as pltpu
from jax.sharding import PartitionSpec as P

B = 64
CB = 24
KP = 8
NCD = 4
GROUP = 8


def shifted(value, axis, steps):
    count = lax.axis_size(axis)
    pairs = [(source, (source + steps) % count) for source in range(count)]
    return lax.ppermute(value, axis, pairs)


def widen(values, left_pad, right_pad):
    return jnp.pad(values, ((0, 0),) * (values.ndim - 1) + ((left_pad, right_pad),))


def slab_kernel(halo_rows, row_count, local_k, wpos_ref, jloc_ref, pb_ref, tb_ref, gt_ref,
                s_ref, xs_ref, w_ref):
    window_slots = 5 * NCD
    row_slots = 3 * NCD
    f32 = jnp.float32
    bf16 = jnp.bfloat16
    upper24 = lax.broadcasted_iota(jnp.int32, (CB, 128), 1) >= B
    upper64 = lax.broadcasted_iota(jnp.int32, (B, 128), 1) >= B
    gt_ref[...] = jnp.zeros(gt_ref.shape, f32)
    w_ref[...] = jnp.zeros(w_ref.shape, bf16)

    def place(dst, slot, lane_group, upper, r, p):
        src = pb_ref[r, :, (p // 2) * 128:(p // 2) * 128 + 128].astype(f32)
        if (p % 2 == 1) != upper:
            src = pltpu.roll(src, B, 1)
        keep = upper24 if upper else jnp.logical_not(upper24)
        rows = pl.ds(pl.multiple_of(slot * CB, 8), CB)
        lanes = slice(lane_group * 128, lane_group * 128 + 128)
        pltpu.store(dst.at[rows, lanes], src, mask=keep)

    def group(g, carry):
        base = g * GROUP
        xs_ref[...] = jnp.zeros(xs_ref.shape, f32)
        for m in range(GROUP):
            r = base + m + halo_rows
            for p in range(KP):
                w = wpos_ref[r * KP + p]
                slot = jnp.clip(w - NCD, 0, row_slots - 1)
                place(xs_ref, slot, m // 2, m % 2 == 1, r, p)
        xsb = xs_ref[...].astype(bf16)
        for k in range(local_k):
            s_ref[...] = jnp.zeros(s_ref.shape, f32)
            for m in range(GROUP):
                r = jloc_ref[(base + m) * local_k + k]
                for p in range(KP):
                    w = wpos_ref[r * KP + p]
                    slot = jnp.clip(w, 0, window_slots - 1)
                    place(s_ref, slot, m // 2, m % 2 == 1, r, p)
            parts = []
            for c in range(GROUP // 4):
                for mm in range(4):
                    t = tb_ref[base + 4 * c + mm].astype(f32)
                    if (k % 2 == 1) != (mm % 2 == 1):
                        t = pltpu.roll(t, B, 1)
                    keep = upper64 if mm % 2 == 1 else jnp.logical_not(upper64)
                    w_ref[mm * B:(mm + 1) * B, (mm // 2) * 128:(mm // 2) * 128 + 128] = jnp.where(
                        keep, t, 0.0
                    ).astype(bf16)
                window = s_ref[:, c * 256:(c + 1) * 256].astype(bf16)
                q = lax.dot_general(
                    window, w_ref[...], (((1,), (1,)), ((), ())), preferred_element_type=f32
                )
                parts.append(q.astype(bf16))
            qt = jnp.concatenate(parts, axis=1)
            gt_ref[...] += lax.dot_general(
                qt, xsb, (((1,), (1,)), ((), ())), preferred_element_type=f32
            )
        return carry

    lax.fori_loop(0, row_count // GROUP, group, 0)


def slab_terms_t(wpos, jloc, pb, tb, halo_rows, row_count):
    local_k = tb.shape[2] // B
    window_width = 5 * NCD * CB
    row_width = 3 * NCD * CB
    kernel = functools.partial(slab_kernel, halo_rows, row_count, local_k)
    flops = 2 * row_count * local_k * (window_width * 256 * B + window_width * row_width * B)
    return pl.pallas_call(
        kernel,
        out_shape=jax.ShapeDtypeStruct((window_width, row_width), jnp.float32),
        in_specs=[
            pl.BlockSpec(memory_space=pltpu.SMEM),
            pl.BlockSpec(memory_space=pltpu.SMEM),
            pl.BlockSpec(memory_space=pltpu.VMEM),
            pl.BlockSpec(memory_space=pltpu.VMEM),
        ],
        out_specs=pl.BlockSpec(memory_space=pltpu.VMEM),
        scratch_shapes=[
            pltpu.VMEM((window_width, GROUP * B), jnp.float32),
            pltpu.VMEM((row_width, GROUP * B), jnp.float32),
            pltpu.VMEM((256, 256), jnp.bfloat16),
        ],
        compiler_params=pltpu.CompilerParams(vmem_limit_bytes=48 * 1024 * 1024),
        cost_estimate=pl.CostEstimate(
            flops=flops,
            bytes_accessed=pb.size * 2 + tb.size * 2 + window_width * row_width * 4,
            transcendentals=0,
        ),
    )(wpos, jloc, pb, tb)


def on_device(tangent_blocks, tangent_columns, prolong_blocks, prolong_columns):
    slab_count = lax.axis_size("blk")
    slab_index = lax.axis_index("blk")
    lane_count = lax.axis_size("lane")
    lane_index = lax.axis_index("lane")
    row_count = prolong_blocks.shape[0]
    halo_rows = row_count // 4
    coarse_width = NCD * CB
    fine_count = row_count * slab_count

    lower_blocks = shifted(prolong_blocks[row_count - halo_rows:], "blk", 1)
    upper_blocks = shifted(prolong_blocks[:halo_rows], "blk", -1)
    lower_columns = shifted(prolong_columns[row_count - halo_rows:], "blk", 1)
    upper_columns = shifted(prolong_columns[:halo_rows], "blk", -1)
    near_blocks = jnp.concatenate([lower_blocks, prolong_blocks, upper_blocks], axis=0)
    near_columns = jnp.concatenate([lower_columns, prolong_columns, upper_columns], axis=0)
    wpos = ((near_columns // NCD - slab_index + 2) % slab_count) * NCD + near_columns % NCD
    wpos = wpos.astype(jnp.int32).reshape(-1)
    jloc = (tangent_columns - slab_index * row_count + halo_rows) % fine_count
    jloc = jnp.clip(jloc, 0, row_count + 2 * halo_rows - 1).astype(jnp.int32).reshape(-1)

    gt = slab_terms_t(wpos, jloc, near_blocks, tangent_blocks, halo_rows, row_count)
    terms = gt.T.reshape(3, NCD, CB, 5 * coarse_width)

    shares = lax.dynamic_index_in_dim(terms, lane_index, axis=1, keepdims=False)
    for step in range(1, lane_count):
        piece = lax.dynamic_index_in_dim(
            terms, (lane_index + step) % lane_count, axis=1, keepdims=False
        )
        shares = shares + shifted(piece, "lane", step)
    from_lower = shifted(shares[2], "blk", 1)
    from_upper = shifted(shares[0], "blk", -1)
    coarse_band = (
        widen(shares[1], coarse_width, coarse_width)
        + widen(from_lower, 0, 2 * coarse_width)
        + widen(from_upper, 2 * coarse_width, 0)
    )
    return coarse_band[None]


def solution(mesh):
    return jax.shard_map(
        on_device,
        mesh=mesh,
        in_specs=(P("blk", None, "lane"), P("blk", "lane"), P("blk", None, None), P("blk", None)),
        out_specs=P(("blk", "lane"), None, None),
        check_vma=False,
    )
```

```python
import functools

import jax
import jax.numpy as jnp
from jax import lax
from jax.experimental import pallas as pl
from jax.experimental.pallas import tpu as pltpu
from jax.sharding import PartitionSpec as P

B = 64
CB = 24
KP = 8
NCD = 4
GROUP = 8


def shifted(value, axis, steps):
    count = lax.axis_size(axis)
    pairs = [(source, (source + steps) % count) for source in range(count)]
    return lax.ppermute(value, axis, pairs)


def widen(values, left_pad, right_pad):
    return jnp.pad(values, ((0, 0),) * (values.ndim - 1) + ((left_pad, right_pad),))


NT = (((1,), (1,)), ((), ()))


def half_masks():
    upper24 = lax.broadcasted_iota(jnp.int32, (CB, 128), 1) >= B
    upper64 = lax.broadcasted_iota(jnp.int32, (B, 128), 1) >= B
    return upper24, upper64


def place(src_ref, r, p, dst, slot, lane_group, upper, upper24, flag=None):
    src = src_ref[r, 0:CB, (p // 2) * 128:(p // 2) * 128 + 128].astype(jnp.float32)
    if (p % 2 == 1) != upper:
        src = pltpu.roll(src, B, 1)
    keep = upper24 if upper else jnp.logical_not(upper24)
    if flag is not None:
        keep = jnp.logical_and(keep, flag)
    rows = pl.ds(pl.multiple_of(slot * CB, 8), CB)
    lanes = slice(lane_group * 128, lane_group * 128 + 128)
    pltpu.store(dst.at[rows, lanes], src, mask=keep)


def place_row_side(pb_ref, wpos_ref, wbase, i, xs_ref, m, upper24, flag=None):
    for p in range(KP):
        slot = jnp.clip(wpos_ref[wbase + p] - NCD, 0, 3 * NCD - 1)
        place(pb_ref, i, p, xs_ref, slot, m // 2, m % 2 == 1, upper24, flag)


def place_window(src_ref, r, wpos_ref, wbase, s_ref, m, upper24, flag=None):
    for p in range(KP):
        slot = jnp.clip(wpos_ref[wbase + p], 0, 5 * NCD - 1)
        place(src_ref, r, p, s_ref, slot, m // 2, m % 2 == 1, upper24, flag)


def chunk_product(s_ref, w_ref, c):
    window = s_ref[:, c * 256:(c + 1) * 256].astype(jnp.bfloat16)
    q = lax.dot_general(window, w_ref[...], NT, preferred_element_type=jnp.float32)
    return q.astype(jnp.bfloat16)


def own_kernel(halo_rows, local_k, wpos_ref, jloc_ref, pb_ref, tb_ref, gt_ref, s_ref, xs_ref, w_ref):
    row_count = pb_ref.shape[0]
    f32 = jnp.float32
    upper24, upper64 = half_masks()
    gt_ref[...] = jnp.zeros(gt_ref.shape, f32)
    w_ref[...] = jnp.zeros(w_ref.shape, jnp.bfloat16)

    def group(g, carry):
        base = g * GROUP
        xs_ref[...] = jnp.zeros(xs_ref.shape, f32)
        for m in range(GROUP):
            place_row_side(pb_ref, wpos_ref, (base + m) * KP, base + m, xs_ref, m, upper24)
        xsb = xs_ref[...].astype(jnp.bfloat16)
        stacked = []
        for k in range(local_k):
            s_ref[...] = jnp.zeros(s_ref.shape, f32)
            for m in range(GROUP):
                r = jloc_ref[(base + m) * local_k + k] - halo_rows
                inside = jnp.logical_and(r >= 0, r < row_count)
                rr = jnp.clip(r, 0, row_count - 1)

                place_window(pb_ref, rr, wpos_ref, rr * KP, s_ref, m, upper24, inside)

            parts = []
            for c in range(GROUP // 4):
                for mm in range(4):
                    t = tb_ref[base + 4 * c + mm].astype(f32)
                    if (k % 2 == 1) != (mm % 2 == 1):
                        t = pltpu.roll(t, B, 1)
                    keep = upper64 if mm % 2 == 1 else jnp.logical_not(upper64)
                    w_ref[mm * B:(mm + 1) * B, (mm // 2) * 128:(mm // 2) * 128 + 128] = jnp.where(
                        keep, t, 0.0
                    ).astype(jnp.bfloat16)
                parts.append(chunk_product(s_ref, w_ref, c))
            stacked.append(jnp.concatenate(parts, axis=1))
        qt = jnp.concatenate(stacked, axis=0)
        both = lax.dot_general(qt, xsb, NT, preferred_element_type=f32)
        width = gt_ref.shape[0]
        total = both[0:width]
        for k in range(1, local_k):
            total = total + both[k * width:(k + 1) * width]
        gt_ref[...] += total
        return carry

    lax.fori_loop(0, row_count // GROUP, group, 0)


def halo_kernel(halo_rows, local_k, count_ref, list_ref, wpos_ref, jloc_ref, pb_ref, lo_ref, up_ref,
                tb_ref, ga_ref, gt_ref, s_ref, xs_ref, w_ref):
    row_count = pb_ref.shape[0]
    f32 = jnp.float32
    upper24, upper64 = half_masks()
    gt_ref[...] = ga_ref[...]

    def group(g, carry):
        s_ref[...] = jnp.zeros(s_ref.shape, f32)
        xs_ref[...] = jnp.zeros(xs_ref.shape, f32)
        parts = []
        for c in range(GROUP // 4):
            for mm in range(4):
                m = 4 * c + mm
                pair = list_ref[g * GROUP + m]
                valid = pair >= 0
                pc = jnp.maximum(pair, 0)
                i = pc // local_k
                k = pc % local_k
                r = jloc_ref[pc]
                t = tb_ref[i].astype(f32)
                same = (k % 2) == (mm % 2)
                t = jnp.where(same, t, pltpu.roll(t, B, 1))
                keep = upper64 if mm % 2 == 1 else jnp.logical_not(upper64)
                keep = jnp.logical_and(keep, valid)
                w_ref[mm * B:(mm + 1) * B, (mm // 2) * 128:(mm // 2) * 128 + 128] = jnp.where(
                    keep, t, 0.0
                ).astype(jnp.bfloat16)

                place_row_side(pb_ref, wpos_ref, (i + halo_rows) * KP, i, xs_ref, m, upper24, valid)
                rl = jnp.clip(r, 0, halo_rows - 1)
                from_lower = jnp.logical_and(valid, r < halo_rows)
                place_window(lo_ref, rl, wpos_ref, r * KP, s_ref, m, upper24, from_lower)
                ru = jnp.clip(r - halo_rows - row_count, 0, halo_rows - 1)
                from_upper = jnp.logical_and(valid, r >= halo_rows + row_count)
                place_window(up_ref, ru, wpos_ref, r * KP, s_ref, m, upper24, from_upper)

            parts.append(chunk_product(s_ref, w_ref, c))
        qt = jnp.concatenate(parts, axis=1)
        xsb = xs_ref[...].astype(jnp.bfloat16)
        gt_ref[...] += lax.dot_general(qt, xsb, NT, preferred_element_type=f32)
        return carry

    lax.fori_loop(0, count_ref[0], group, 0)


def scratch():
    return [
        pltpu.VMEM((5 * NCD * CB, GROUP * B), jnp.float32),
        pltpu.VMEM((3 * NCD * CB, GROUP * B), jnp.float32),
        pltpu.VMEM((256, 256), jnp.bfloat16),
    ]


def own_terms(wpos_own, jloc, pb, tb, halo_rows):
    local_k = tb.shape[2] // B
    row_count = pb.shape[0]
    shape = (5 * NCD * CB, 3 * NCD * CB)
    flops = 2 * row_count * local_k * shape[0] * (256 + shape[1]) * B
    smem = pl.BlockSpec(memory_space=pltpu.SMEM)
    vmem = pl.BlockSpec(memory_space=pltpu.VMEM)
    return pl.pallas_call(
        functools.partial(own_kernel, halo_rows, local_k),
        out_shape=jax.ShapeDtypeStruct(shape, jnp.float32),
        in_specs=[smem, smem, vmem, vmem],
        out_specs=vmem,
        scratch_shapes=scratch(),
        compiler_params=pltpu.CompilerParams(vmem_limit_bytes=48 * 1024 * 1024),
        cost_estimate=pl.CostEstimate(
            flops=flops, bytes_accessed=pb.size * 2 + tb.size * 2 + shape[0] * shape[1] * 4,
            transcendentals=0,
        ),
    )(wpos_own, jloc, pb, tb)


def halo_terms(count, pair_list, wpos, jloc, pb, lower, upper, tb, own_part, halo_rows):
    local_k = tb.shape[2] // B
    shape = own_part.shape
    smem = pl.BlockSpec(memory_space=pltpu.SMEM)
    vmem = pl.BlockSpec(memory_space=pltpu.VMEM)
    flops = 2 * pair_list.shape[0] // 2 * shape[0] * (256 + shape[1]) * B
    return pl.pallas_call(
        functools.partial(halo_kernel, halo_rows, local_k),
        out_shape=jax.ShapeDtypeStruct(shape, jnp.float32),
        in_specs=[smem, smem, smem, smem, vmem, vmem, vmem, vmem, vmem],
        out_specs=vmem,
        scratch_shapes=scratch(),
        compiler_params=pltpu.CompilerParams(vmem_limit_bytes=48 * 1024 * 1024),
        cost_estimate=pl.CostEstimate(
            flops=flops, bytes_accessed=pb.size * 2 + tb.size * 2 + shape[0] * shape[1] * 8,
            transcendentals=0,
        ),
    )(count, pair_list, wpos, jloc, pb, lower, upper, tb, own_part)


def on_device(tangent_blocks, tangent_columns, prolong_blocks, prolong_columns):
    slab_count = lax.axis_size("blk")
    slab_index = lax.axis_index("blk")
    lane_count = lax.axis_size("lane")
    lane_index = lax.axis_index("lane")
    row_count = prolong_blocks.shape[0]
    halo_rows = row_count // 4
    coarse_width = NCD * CB
    fine_count = row_count * slab_count

    def with_columns(rows):
        blocks = prolong_blocks[rows]
        columns = prolong_columns[rows].astype(jnp.bfloat16)
        columns = jnp.pad(columns, ((0, 0), (0, blocks.shape[2] - KP)))[:, None, :]
        return jnp.concatenate([blocks, columns], axis=1)

    lower = shifted(with_columns(slice(row_count - halo_rows, row_count)), "blk", 1)
    upper = shifted(with_columns(slice(0, halo_rows)), "blk", -1)

    def window_slots(columns):
        slots = ((columns // NCD - slab_index + 2) % slab_count) * NCD + columns % NCD
        return slots.astype(jnp.int32)

    wpos_own = window_slots(prolong_columns)
    jloc = (tangent_columns - slab_index * row_count + halo_rows) % fine_count
    jloc = jnp.clip(jloc, 0, row_count + 2 * halo_rows - 1).astype(jnp.int32).reshape(-1)

    own_part = own_terms(wpos_own.reshape(-1), jloc, prolong_blocks, tangent_blocks, halo_rows)

    pair_count = jloc.shape[0]
    in_halo = jnp.logical_or(jloc < halo_rows, jloc >= halo_rows + row_count)
    order = jnp.cumsum(in_halo.astype(jnp.int32)) - 1
    slots = jnp.arange(pair_count, dtype=jnp.int32)
    match = jnp.logical_and(in_halo[None, :], order[None, :] == slots[:, None])
    pair_list = jnp.where(
        jnp.any(match, axis=1), jnp.sum(jnp.where(match, slots[None, :], 0), axis=1), -1
    ).astype(jnp.int32)
    halo_count = jnp.sum(in_halo.astype(jnp.int32))
    group_count = ((halo_count + GROUP - 1) // GROUP).astype(jnp.int32).reshape(1)

    lower_columns = lower[:, CB, :KP].astype(jnp.int32)
    upper_columns = upper[:, CB, :KP].astype(jnp.int32)
    wpos = jnp.concatenate(
        [window_slots(lower_columns), wpos_own, window_slots(upper_columns)], axis=0
    ).reshape(-1)
    gt = halo_terms(group_count, pair_list, wpos, jloc, prolong_blocks, lower, upper,
                    tangent_blocks, own_part, halo_rows)
    terms = gt.T.reshape(3, NCD, CB, 5 * coarse_width)

    shares = lax.dynamic_index_in_dim(terms, lane_index, axis=1, keepdims=False)
    for step in range(1, lane_count):
        piece = lax.dynamic_index_in_dim(
            terms, (lane_index + step) % lane_count, axis=1, keepdims=False
        )
        shares = shares + shifted(piece, "lane", step)
    from_lower = shifted(shares[2], "blk", 1)
    from_upper = shifted(shares[0], "blk", -1)
    coarse_band = (
        widen(shares[1], coarse_width, coarse_width)
        + widen(from_lower, 0, 2 * coarse_width)
        + widen(from_upper, 2 * coarse_width, 0)
    )
    return coarse_band[None]


def solution(mesh):
    return jax.shard_map(
        on_device,
        mesh=mesh,
        in_specs=(P("blk", None, "lane"), P("blk", "lane"), P("blk", None, None), P("blk", None)),
        out_specs=P(("blk", "lane"), None, None),
        check_vma=False,
    )
```

```python
import functools

import jax
import jax.numpy as jnp
from jax import lax
from jax.experimental import pallas as pl
from jax.experimental.pallas import tpu as pltpu
from jax.sharding import PartitionSpec as P

B = 64
CB = 24
KP = 8
NCD = 4
GROUP = 8


def shifted(value, axis, steps):
    count = lax.axis_size(axis)
    pairs = [(source, (source + steps) % count) for source in range(count)]
    return lax.ppermute(value, axis, pairs)


def widen(values, left_pad, right_pad):
    return jnp.pad(values, ((0, 0),) * (values.ndim - 1) + ((left_pad, right_pad),))


def slab_kernel(halo_rows, row_count, local_k, wpos_ref, jloc_ref, lower_ref, own_ref, upper_ref,
                tb_ref, gt_ref, pb_ref, s_ref, xs_ref, w_ref, sems):
    copies = [
        pltpu.make_async_copy(lower_ref, pb_ref.at[0:halo_rows], sems.at[0]),
        pltpu.make_async_copy(own_ref, pb_ref.at[halo_rows:halo_rows + row_count], sems.at[1]),
        pltpu.make_async_copy(
            upper_ref, pb_ref.at[halo_rows + row_count:2 * halo_rows + row_count], sems.at[2]
        ),
    ]
    for copy in copies:
        copy.start()
    window_slots = 5 * NCD
    row_slots = 3 * NCD
    f32 = jnp.float32
    bf16 = jnp.bfloat16
    upper24 = lax.broadcasted_iota(jnp.int32, (CB, 128), 1) >= B
    upper64 = lax.broadcasted_iota(jnp.int32, (B, 128), 1) >= B
    gt_ref[...] = jnp.zeros(gt_ref.shape, f32)
    w_ref[...] = jnp.zeros(w_ref.shape, bf16)
    for copy in copies:
        copy.wait()

    def place(dst, slot, lane_group, upper, r, p):
        src = pb_ref[r, :, (p // 2) * 128:(p // 2) * 128 + 128].astype(f32)
        if (p % 2 == 1) != upper:
            src = pltpu.roll(src, B, 1)
        keep = upper24 if upper else jnp.logical_not(upper24)
        rows = pl.ds(pl.multiple_of(slot * CB, 8), CB)
        lanes = slice(lane_group * 128, lane_group * 128 + 128)
        pltpu.store(dst.at[rows, lanes], src, mask=keep)

    def group(g, carry):
        base = g * GROUP
        xs_ref[...] = jnp.zeros(xs_ref.shape, f32)
        for m in range(GROUP):
            r = base + m + halo_rows
            for p in range(KP):
                w = wpos_ref[r * KP + p]
                slot = jnp.clip(w - NCD, 0, row_slots - 1)
                place(xs_ref, slot, m // 2, m % 2 == 1, r, p)
        xsb = xs_ref[...].astype(bf16)
        for k in range(local_k):
            s_ref[...] = jnp.zeros(s_ref.shape, f32)
            for m in range(GROUP):
                r = jloc_ref[(base + m) * local_k + k]
                for p in range(KP):
                    w = wpos_ref[r * KP + p]
                    slot = jnp.clip(w, 0, window_slots - 1)
                    place(s_ref, slot, m // 2, m % 2 == 1, r, p)
            parts = []
            for c in range(GROUP // 4):
                for mm in range(4):
                    t = tb_ref[base + 4 * c + mm].astype(f32)
                    if (k % 2 == 1) != (mm % 2 == 1):
                        t = pltpu.roll(t, B, 1)
                    keep = upper64 if mm % 2 == 1 else jnp.logical_not(upper64)
                    w_ref[mm * B:(mm + 1) * B, (mm // 2) * 128:(mm // 2) * 128 + 128] = jnp.where(
                        keep, t, 0.0
                    ).astype(bf16)
                window = s_ref[:, c * 256:(c + 1) * 256].astype(bf16)
                q = lax.dot_general(
                    window, w_ref[...], (((1,), (1,)), ((), ())), preferred_element_type=f32
                )
                parts.append(q.astype(bf16))
            qt = jnp.concatenate(parts, axis=1)
            gt_ref[...] += lax.dot_general(
                qt, xsb, (((1,), (1,)), ((), ())), preferred_element_type=f32
            )
        return carry

    lax.fori_loop(0, row_count // GROUP, group, 0)


def slab_terms_t(wpos, jloc, lower, own, upper, tb, halo_rows, row_count):
    local_k = tb.shape[2] // B
    window_width = 5 * NCD * CB
    row_width = 3 * NCD * CB
    kernel = functools.partial(slab_kernel, halo_rows, row_count, local_k)
    flops = 2 * row_count * local_k * (window_width * 256 * B + window_width * row_width * B)
    return pl.pallas_call(
        kernel,
        out_shape=jax.ShapeDtypeStruct((window_width, row_width), jnp.float32),
        in_specs=[
            pl.BlockSpec(memory_space=pltpu.SMEM),
            pl.BlockSpec(memory_space=pltpu.SMEM),
            pl.BlockSpec(memory_space=pl.ANY),
            pl.BlockSpec(memory_space=pl.ANY),
            pl.BlockSpec(memory_space=pl.ANY),
            pl.BlockSpec(memory_space=pltpu.VMEM),
        ],
        out_specs=pl.BlockSpec(memory_space=pltpu.VMEM),
        scratch_shapes=[
            pltpu.VMEM((row_count + 2 * halo_rows,) + own.shape[1:], own.dtype),
            pltpu.VMEM((window_width, GROUP * B), jnp.float32),
            pltpu.VMEM((row_width, GROUP * B), jnp.float32),
            pltpu.VMEM((256, 256), jnp.bfloat16),
            pltpu.SemaphoreType.DMA((3,)),
        ],
        compiler_params=pltpu.CompilerParams(vmem_limit_bytes=48 * 1024 * 1024),
        cost_estimate=pl.CostEstimate(
            flops=flops,
            bytes_accessed=(lower.size + own.size + upper.size) * 2 + tb.size * 2 + window_width * row_width * 4,
            transcendentals=0,
        ),
    )(wpos, jloc, lower, own, upper, tb)


def on_device(tangent_blocks, tangent_columns, prolong_blocks, prolong_columns):
    slab_count = lax.axis_size("blk")
    slab_index = lax.axis_index("blk")
    lane_count = lax.axis_size("lane")
    lane_index = lax.axis_index("lane")
    row_count = prolong_blocks.shape[0]
    halo_rows = row_count // 4
    coarse_width = NCD * CB
    fine_count = row_count * slab_count

    lower_blocks = shifted(prolong_blocks[row_count - halo_rows:], "blk", 1)
    upper_blocks = shifted(prolong_blocks[:halo_rows], "blk", -1)
    lower_columns = shifted(prolong_columns[row_count - halo_rows:], "blk", 1)
    upper_columns = shifted(prolong_columns[:halo_rows], "blk", -1)
    near_columns = jnp.concatenate([lower_columns, prolong_columns, upper_columns], axis=0)
    wpos = ((near_columns // NCD - slab_index + 2) % slab_count) * NCD + near_columns % NCD
    wpos = wpos.astype(jnp.int32).reshape(-1)
    jloc = (tangent_columns - slab_index * row_count + halo_rows) % fine_count
    jloc = jnp.clip(jloc, 0, row_count + 2 * halo_rows - 1).astype(jnp.int32).reshape(-1)

    gt = slab_terms_t(wpos, jloc, lower_blocks, prolong_blocks, upper_blocks, tangent_blocks,
                      halo_rows, row_count)
    terms = gt.T.reshape(3, NCD, CB, 5 * coarse_width)

    shares = lax.dynamic_index_in_dim(terms, lane_index, axis=1, keepdims=False)
    for step in range(1, lane_count):
        piece = lax.dynamic_index_in_dim(
            terms, (lane_index + step) % lane_count, axis=1, keepdims=False
        )
        shares = shares + shifted(piece, "lane", step)
    from_lower = shifted(shares[2], "blk", 1)
    from_upper = shifted(shares[0], "blk", -1)
    coarse_band = (
        widen(shares[1], coarse_width, coarse_width)
        + widen(from_lower, 0, 2 * coarse_width)
        + widen(from_upper, 2 * coarse_width, 0)
    )
    return coarse_band[None]


def solution(mesh):
    return jax.shard_map(
        on_device,
        mesh=mesh,
        in_specs=(P("blk", None, "lane"), P("blk", "lane"), P("blk", None, None), P("blk", None)),
        out_specs=P(("blk", "lane"), None, None),
        check_vma=False,
    )
```

```python
import functools

import jax
import jax.numpy as jnp
from jax import lax
from jax.experimental import pallas as pl
from jax.experimental.pallas import tpu as pltpu
from jax.sharding import PartitionSpec as P

B = 64
CB = 24
KP = 8
NCD = 4
GROUP = 8


def shifted(value, axis, steps):
    count = lax.axis_size(axis)
    pairs = [(source, (source + steps) % count) for source in range(count)]
    return lax.ppermute(value, axis, pairs)


def widen(values, left_pad, right_pad):
    return jnp.pad(values, ((0, 0),) * (values.ndim - 1) + ((left_pad, right_pad),))


def row_side_kernel(wpos_ref, own_ref, out_ref, xs_ref):
    f32 = jnp.float32
    upper24 = lax.broadcasted_iota(jnp.int32, (CB, 128), 1) >= B
    row_slots = 3 * NCD

    def group(g, carry):
        base = g * GROUP
        xs_ref[...] = jnp.zeros(xs_ref.shape, f32)
        for m in range(GROUP):
            upper = m % 2 == 1
            for p in range(KP):
                slot = jnp.clip(wpos_ref[(base + m) * KP + p] - NCD, 0, row_slots - 1)
                src = own_ref[base + m, :, (p // 2) * 128:(p // 2) * 128 + 128].astype(f32)
                if (p % 2 == 1) != upper:
                    src = pltpu.roll(src, B, 1)
                keep = upper24 if upper else jnp.logical_not(upper24)
                rows = pl.ds(pl.multiple_of(slot * CB, 8), CB)
                lanes = slice((m // 2) * 128, (m // 2) * 128 + 128)
                pltpu.store(xs_ref.at[rows, lanes], src, mask=keep)
        out_ref[g] = xs_ref[...].astype(jnp.bfloat16)
        return carry

    lax.fori_loop(0, out_ref.shape[0], group, 0)


def row_side(wpos_own, own):
    row_count = own.shape[0]
    groups = row_count // GROUP
    shape = (groups, 3 * NCD * CB, GROUP * B)
    return pl.pallas_call(
        row_side_kernel,
        out_shape=jax.ShapeDtypeStruct(shape, jnp.bfloat16),
        in_specs=[pl.BlockSpec(memory_space=pltpu.SMEM), pl.BlockSpec(memory_space=pltpu.VMEM)],
        out_specs=pl.BlockSpec(memory_space=pltpu.VMEM),
        scratch_shapes=[pltpu.VMEM(shape[1:], jnp.float32)],
        compiler_params=pltpu.CompilerParams(vmem_limit_bytes=48 * 1024 * 1024),
        cost_estimate=pl.CostEstimate(
            flops=0, bytes_accessed=own.size * 2 + groups * shape[1] * shape[2] * 2,
            transcendentals=0,
        ),
    )(wpos_own, own)


def slab_kernel(halo_rows, row_count, local_k, wpos_ref, jloc_ref, lower_ref, own_ref, upper_ref,
                tb_ref, xsall_ref, gt_ref, pb_ref, s_ref, w_ref, sems):
    copies = [
        pltpu.make_async_copy(lower_ref, pb_ref.at[0:halo_rows], sems.at[0]),
        pltpu.make_async_copy(own_ref, pb_ref.at[halo_rows:halo_rows + row_count], sems.at[1]),
        pltpu.make_async_copy(
            upper_ref, pb_ref.at[halo_rows + row_count:2 * halo_rows + row_count], sems.at[2]
        ),
    ]
    for copy in copies:
        copy.start()
    window_slots = 5 * NCD
    row_slots = 3 * NCD
    f32 = jnp.float32
    bf16 = jnp.bfloat16
    upper24 = lax.broadcasted_iota(jnp.int32, (CB, 128), 1) >= B
    upper64 = lax.broadcasted_iota(jnp.int32, (B, 128), 1) >= B
    gt_ref[...] = jnp.zeros(gt_ref.shape, f32)
    w_ref[...] = jnp.zeros(w_ref.shape, bf16)
    for copy in copies:
        copy.wait()

    def place(dst, slot, lane_group, upper, r, p):
        src = pb_ref[r, :, (p // 2) * 128:(p // 2) * 128 + 128].astype(f32)
        if (p % 2 == 1) != upper:
            src = pltpu.roll(src, B, 1)
        keep = upper24 if upper else jnp.logical_not(upper24)
        rows = pl.ds(pl.multiple_of(slot * CB, 8), CB)
        lanes = slice(lane_group * 128, lane_group * 128 + 128)
        pltpu.store(dst.at[rows, lanes], src, mask=keep)

    def group(g, carry):
        base = g * GROUP
        xsb = xsall_ref[g]
        for k in range(local_k):
            s_ref[...] = jnp.zeros(s_ref.shape, f32)
            for m in range(GROUP):
                r = jloc_ref[(base + m) * local_k + k]
                for p in range(KP):
                    w = wpos_ref[r * KP + p]
                    slot = jnp.clip(w, 0, window_slots - 1)
                    place(s_ref, slot, m // 2, m % 2 == 1, r, p)
            parts = []
            for c in range(GROUP // 4):
                for mm in range(4):
                    t = tb_ref[base + 4 * c + mm].astype(f32)
                    if (k % 2 == 1) != (mm % 2 == 1):
                        t = pltpu.roll(t, B, 1)
                    keep = upper64 if mm % 2 == 1 else jnp.logical_not(upper64)
                    w_ref[mm * B:(mm + 1) * B, (mm // 2) * 128:(mm // 2) * 128 + 128] = jnp.where(
                        keep, t, 0.0
                    ).astype(bf16)
                window = s_ref[:, c * 256:(c + 1) * 256].astype(bf16)
                q = lax.dot_general(
                    window, w_ref[...], (((1,), (1,)), ((), ())), preferred_element_type=f32
                )
                parts.append(q.astype(bf16))
            qt = jnp.concatenate(parts, axis=1)
            gt_ref[...] += lax.dot_general(
                qt, xsb, (((1,), (1,)), ((), ())), preferred_element_type=f32
            )
        return carry

    lax.fori_loop(0, row_count // GROUP, group, 0)


def slab_terms_t(wpos, jloc, lower, own, upper, tb, xs_all, halo_rows, row_count):
    local_k = tb.shape[2] // B
    window_width = 5 * NCD * CB
    row_width = 3 * NCD * CB
    kernel = functools.partial(slab_kernel, halo_rows, row_count, local_k)
    flops = 2 * row_count * local_k * (window_width * 256 * B + window_width * row_width * B)
    return pl.pallas_call(
        kernel,
        out_shape=jax.ShapeDtypeStruct((window_width, row_width), jnp.float32),
        in_specs=[
            pl.BlockSpec(memory_space=pltpu.SMEM),
            pl.BlockSpec(memory_space=pltpu.SMEM),
            pl.BlockSpec(memory_space=pl.ANY),
            pl.BlockSpec(memory_space=pl.ANY),
            pl.BlockSpec(memory_space=pl.ANY),
            pl.BlockSpec(memory_space=pltpu.VMEM),
            pl.BlockSpec(memory_space=pltpu.VMEM),
        ],
        out_specs=pl.BlockSpec(memory_space=pltpu.VMEM),
        scratch_shapes=[
            pltpu.VMEM((row_count + 2 * halo_rows,) + own.shape[1:], own.dtype),
            pltpu.VMEM((window_width, GROUP * B), jnp.float32),
            pltpu.VMEM((256, 256), jnp.bfloat16),
            pltpu.SemaphoreType.DMA((3,)),
        ],
        compiler_params=pltpu.CompilerParams(vmem_limit_bytes=48 * 1024 * 1024),
        cost_estimate=pl.CostEstimate(
            flops=flops,
            bytes_accessed=(lower.size + own.size + upper.size) * 2 + tb.size * 2 + window_width * row_width * 4,
            transcendentals=0,
        ),
    )(wpos, jloc, lower, own, upper, tb, xs_all)


def on_device(tangent_blocks, tangent_columns, prolong_blocks, prolong_columns):
    slab_count = lax.axis_size("blk")
    slab_index = lax.axis_index("blk")
    lane_count = lax.axis_size("lane")
    lane_index = lax.axis_index("lane")
    row_count = prolong_blocks.shape[0]
    halo_rows = row_count // 4
    coarse_width = NCD * CB
    fine_count = row_count * slab_count

    lower_blocks = shifted(prolong_blocks[row_count - halo_rows:], "blk", 1)
    upper_blocks = shifted(prolong_blocks[:halo_rows], "blk", -1)
    lower_columns = shifted(prolong_columns[row_count - halo_rows:], "blk", 1)
    upper_columns = shifted(prolong_columns[:halo_rows], "blk", -1)
    near_columns = jnp.concatenate([lower_columns, prolong_columns, upper_columns], axis=0)
    wpos = ((near_columns // NCD - slab_index + 2) % slab_count) * NCD + near_columns % NCD
    wpos = wpos.astype(jnp.int32).reshape(-1)
    jloc = (tangent_columns - slab_index * row_count + halo_rows) % fine_count
    jloc = jnp.clip(jloc, 0, row_count + 2 * halo_rows - 1).astype(jnp.int32).reshape(-1)

    own_slots = ((prolong_columns // NCD - slab_index + 2) % slab_count) * NCD + prolong_columns % NCD
    xs_all = row_side(own_slots.astype(jnp.int32).reshape(-1), prolong_blocks)
    gt = slab_terms_t(wpos, jloc, lower_blocks, prolong_blocks, upper_blocks, tangent_blocks,
                      xs_all, halo_rows, row_count)
    terms = gt.T.reshape(3, NCD, CB, 5 * coarse_width)

    shares = lax.dynamic_index_in_dim(terms, lane_index, axis=1, keepdims=False)
    for step in range(1, lane_count):
        piece = lax.dynamic_index_in_dim(
            terms, (lane_index + step) % lane_count, axis=1, keepdims=False
        )
        shares = shares + shifted(piece, "lane", step)
    from_lower = shifted(shares[2], "blk", 1)
    from_upper = shifted(shares[0], "blk", -1)
    coarse_band = (
        widen(shares[1], coarse_width, coarse_width)
        + widen(from_lower, 0, 2 * coarse_width)
        + widen(from_upper, 2 * coarse_width, 0)
    )
    return coarse_band[None]


def solution(mesh):
    return jax.shard_map(
        on_device,
        mesh=mesh,
        in_specs=(P("blk", None, "lane"), P("blk", "lane"), P("blk", None, None), P("blk", None)),
        out_specs=P(("blk", "lane"), None, None),
        check_vma=False,
    )
```

```python
import functools

import jax
import jax.numpy as jnp
from jax import lax
from jax.experimental import pallas as pl
from jax.experimental.pallas import tpu as pltpu
from jax.sharding import PartitionSpec as P

B = 64
CB = 24
KP = 8
NCD = 4
GROUP = 8


def shifted(value, axis, steps):
    count = lax.axis_size(axis)
    pairs = [(source, (source + steps) % count) for source in range(count)]
    return lax.ppermute(value, axis, pairs)


def widen(values, left_pad, right_pad):
    return jnp.pad(values, ((0, 0),) * (values.ndim - 1) + ((left_pad, right_pad),))


def slab_kernel(halo_rows, row_count, local_k, wpos_ref, jloc_ref, lower_ref, own_ref, upper_ref,
                tb_ref, gt_ref, pb_ref, s_ref, xs_ref, w_ref, qall_ref, xall_ref, sems):
    copies = [
        pltpu.make_async_copy(lower_ref, pb_ref.at[0:halo_rows], sems.at[0]),
        pltpu.make_async_copy(own_ref, pb_ref.at[halo_rows:halo_rows + row_count], sems.at[1]),
        pltpu.make_async_copy(
            upper_ref, pb_ref.at[halo_rows + row_count:2 * halo_rows + row_count], sems.at[2]
        ),
    ]
    for copy in copies:
        copy.start()
    window_slots = 5 * NCD
    row_slots = 3 * NCD
    f32 = jnp.float32
    bf16 = jnp.bfloat16
    upper24 = lax.broadcasted_iota(jnp.int32, (CB, 128), 1) >= B
    upper64 = lax.broadcasted_iota(jnp.int32, (B, 128), 1) >= B
    gt_ref[...] = jnp.zeros(gt_ref.shape, f32)
    w_ref[...] = jnp.zeros(w_ref.shape, bf16)
    for copy in copies:
        copy.wait()

    def place(dst, slot, lane_group, upper, r, p):
        src = pb_ref[r, :, (p // 2) * 128:(p // 2) * 128 + 128].astype(f32)
        if (p % 2 == 1) != upper:
            src = pltpu.roll(src, B, 1)
        keep = upper24 if upper else jnp.logical_not(upper24)
        rows = pl.ds(pl.multiple_of(slot * CB, 8), CB)
        lanes = slice(lane_group * 128, lane_group * 128 + 128)
        pltpu.store(dst.at[rows, lanes], src, mask=keep)

    def group(g, carry):
        base = g * GROUP
        xs_ref[...] = jnp.zeros(xs_ref.shape, f32)
        for m in range(GROUP):
            r = base + m + halo_rows
            for p in range(KP):
                w = wpos_ref[r * KP + p]
                slot = jnp.clip(w - NCD, 0, row_slots - 1)
                place(xs_ref, slot, m // 2, m % 2 == 1, r, p)
        xsb = xs_ref[...].astype(bf16)
        span = pl.ds(pl.multiple_of(g * GROUP * B, GROUP * B), GROUP * B)
        xall_ref[:, span] = xsb
        for k in range(local_k):
            s_ref[...] = jnp.zeros(s_ref.shape, f32)
            for m in range(GROUP):
                r = jloc_ref[(base + m) * local_k + k]
                for p in range(KP):
                    w = wpos_ref[r * KP + p]
                    slot = jnp.clip(w, 0, window_slots - 1)
                    place(s_ref, slot, m // 2, m % 2 == 1, r, p)
            parts = []
            for c in range(GROUP // 4):
                for mm in range(4):
                    t = tb_ref[base + 4 * c + mm].astype(f32)
                    if (k % 2 == 1) != (mm % 2 == 1):
                        t = pltpu.roll(t, B, 1)
                    keep = upper64 if mm % 2 == 1 else jnp.logical_not(upper64)
                    w_ref[mm * B:(mm + 1) * B, (mm // 2) * 128:(mm // 2) * 128 + 128] = jnp.where(
                        keep, t, 0.0
                    ).astype(bf16)
                window = s_ref[:, c * 256:(c + 1) * 256].astype(bf16)
                q = lax.dot_general(
                    window, w_ref[...], (((1,), (1,)), ((), ())), preferred_element_type=f32
                )
                parts.append(q.astype(bf16))
            qall_ref[k, :, span] = jnp.concatenate(parts, axis=1)
        return carry

    lax.fori_loop(0, row_count // GROUP, group, 0)
    total = lax.dot_general(qall_ref[0], xall_ref[...], (((1,), (1,)), ((), ())),
                            preferred_element_type=f32)
    for k in range(1, local_k):
        total = total + lax.dot_general(qall_ref[k], xall_ref[...], (((1,), (1,)), ((), ())),
                                        preferred_element_type=f32)
    gt_ref[...] = total


def slab_terms_t(wpos, jloc, lower, own, upper, tb, halo_rows, row_count):
    local_k = tb.shape[2] // B
    window_width = 5 * NCD * CB
    row_width = 3 * NCD * CB
    kernel = functools.partial(slab_kernel, halo_rows, row_count, local_k)
    flops = 2 * row_count * local_k * (window_width * 256 * B + window_width * row_width * B)
    return pl.pallas_call(
        kernel,
        out_shape=jax.ShapeDtypeStruct((window_width, row_width), jnp.float32),
        in_specs=[
            pl.BlockSpec(memory_space=pltpu.SMEM),
            pl.BlockSpec(memory_space=pltpu.SMEM),
            pl.BlockSpec(memory_space=pl.ANY),
            pl.BlockSpec(memory_space=pl.ANY),
            pl.BlockSpec(memory_space=pl.ANY),
            pl.BlockSpec(memory_space=pltpu.VMEM),
        ],
        out_specs=pl.BlockSpec(memory_space=pltpu.VMEM),
        scratch_shapes=[
            pltpu.VMEM((row_count + 2 * halo_rows,) + own.shape[1:], own.dtype),
            pltpu.VMEM((window_width, GROUP * B), jnp.float32),
            pltpu.VMEM((row_width, GROUP * B), jnp.float32),
            pltpu.VMEM((256, 256), jnp.bfloat16),
            pltpu.VMEM((local_k, window_width, row_count * B), jnp.bfloat16),
            pltpu.VMEM((row_width, row_count * B), jnp.bfloat16),
            pltpu.SemaphoreType.DMA((3,)),
        ],
        compiler_params=pltpu.CompilerParams(vmem_limit_bytes=60 * 1024 * 1024),
        cost_estimate=pl.CostEstimate(
            flops=flops,
            bytes_accessed=(lower.size + own.size + upper.size) * 2 + tb.size * 2 + window_width * row_width * 4,
            transcendentals=0,
        ),
    )(wpos, jloc, lower, own, upper, tb)


def on_device(tangent_blocks, tangent_columns, prolong_blocks, prolong_columns):
    slab_count = lax.axis_size("blk")
    slab_index = lax.axis_index("blk")
    lane_count = lax.axis_size("lane")
    lane_index = lax.axis_index("lane")
    row_count = prolong_blocks.shape[0]
    halo_rows = row_count // 4
    coarse_width = NCD * CB
    fine_count = row_count * slab_count

    lower_blocks = shifted(prolong_blocks[row_count - halo_rows:], "blk", 1)
    upper_blocks = shifted(prolong_blocks[:halo_rows], "blk", -1)
    lower_columns = shifted(prolong_columns[row_count - halo_rows:], "blk", 1)
    upper_columns = shifted(prolong_columns[:halo_rows], "blk", -1)
    near_columns = jnp.concatenate([lower_columns, prolong_columns, upper_columns], axis=0)
    wpos = ((near_columns // NCD - slab_index + 2) % slab_count) * NCD + near_columns % NCD
    wpos = wpos.astype(jnp.int32).reshape(-1)
    jloc = (tangent_columns - slab_index * row_count + halo_rows) % fine_count
    jloc = jnp.clip(jloc, 0, row_count + 2 * halo_rows - 1).astype(jnp.int32).reshape(-1)

    gt = slab_terms_t(wpos, jloc, lower_blocks, prolong_blocks, upper_blocks, tangent_blocks,
                      halo_rows, row_count)
    terms = gt.T.reshape(3, NCD, CB, 5 * coarse_width)

    shares = lax.dynamic_index_in_dim(terms, lane_index, axis=1, keepdims=False)
    for step in range(1, lane_count):
        piece = lax.dynamic_index_in_dim(
            terms, (lane_index + step) % lane_count, axis=1, keepdims=False
        )
        shares = shares + shifted(piece, "lane", step)
    from_lower = shifted(shares[2], "blk", 1)
    from_upper = shifted(shares[0], "blk", -1)
    coarse_band = (
        widen(shares[1], coarse_width, coarse_width)
        + widen(from_lower, 0, 2 * coarse_width)
        + widen(from_upper, 2 * coarse_width, 0)
    )
    return coarse_band[None]


def solution(mesh):
    return jax.shard_map(
        on_device,
        mesh=mesh,
        in_specs=(P("blk", None, "lane"), P("blk", "lane"), P("blk", None, None), P("blk", None)),
        out_specs=P(("blk", "lane"), None, None),
        check_vma=False,
    )
```

```python
import functools

import jax
import jax.numpy as jnp
from jax import lax
from jax.experimental import pallas as pl
from jax.experimental.pallas import tpu as pltpu
from jax.sharding import PartitionSpec as P

B = 64
CB = 24
KP = 8
NCD = 4
GROUP = 8


def shifted(value, axis, steps):
    count = lax.axis_size(axis)
    pairs = [(source, (source + steps) % count) for source in range(count)]
    return lax.ppermute(value, axis, pairs)


def widen(values, left_pad, right_pad):
    return jnp.pad(values, ((0, 0),) * (values.ndim - 1) + ((left_pad, right_pad),))


def send_rows_kernel(halo_rows, src_ref, tail_ref, head_ref, sems):
    row_count = src_ref.shape[0]
    copies = [
        pltpu.make_async_copy(src_ref.at[row_count - halo_rows:row_count], tail_ref, sems.at[0]),
        pltpu.make_async_copy(src_ref.at[0:halo_rows], head_ref, sems.at[1]),
    ]
    for copy in copies:
        copy.start()
    for copy in copies:
        copy.wait()


def send_rows(blocks, halo_rows):
    piece = jax.ShapeDtypeStruct((halo_rows,) + blocks.shape[1:], blocks.dtype)
    return pl.pallas_call(
        functools.partial(send_rows_kernel, halo_rows),
        out_shape=(piece, piece),
        in_specs=[pl.BlockSpec(memory_space=pl.ANY)],
        out_specs=(pl.BlockSpec(memory_space=pl.ANY), pl.BlockSpec(memory_space=pl.ANY)),
        scratch_shapes=[pltpu.SemaphoreType.DMA((2,))],
        cost_estimate=pl.CostEstimate(
            flops=0, bytes_accessed=4 * halo_rows * blocks[0].size * 2, transcendentals=0
        ),
    )(blocks)


def slab_kernel(halo_rows, row_count, local_k, wpos_ref, jloc_ref, lower_ref, own_ref, upper_ref,
                tb_ref, gt_ref, pb_ref, s_ref, xs_ref, w_ref, sems):
    copies = [
        pltpu.make_async_copy(lower_ref, pb_ref.at[0:halo_rows], sems.at[0]),
        pltpu.make_async_copy(own_ref, pb_ref.at[halo_rows:halo_rows + row_count], sems.at[1]),
        pltpu.make_async_copy(
            upper_ref, pb_ref.at[halo_rows + row_count:2 * halo_rows + row_count], sems.at[2]
        ),
    ]
    for copy in copies:
        copy.start()
    window_slots = 5 * NCD
    row_slots = 3 * NCD
    f32 = jnp.float32
    bf16 = jnp.bfloat16
    upper24 = lax.broadcasted_iota(jnp.int32, (CB, 128), 1) >= B
    upper64 = lax.broadcasted_iota(jnp.int32, (B, 128), 1) >= B
    gt_ref[...] = jnp.zeros(gt_ref.shape, f32)
    w_ref[...] = jnp.zeros(w_ref.shape, bf16)
    for copy in copies:
        copy.wait()

    def place(dst, slot, lane_group, upper, r, p):
        src = pb_ref[r, :, (p // 2) * 128:(p // 2) * 128 + 128].astype(f32)
        if (p % 2 == 1) != upper:
            src = pltpu.roll(src, B, 1)
        keep = upper24 if upper else jnp.logical_not(upper24)
        rows = pl.ds(pl.multiple_of(slot * CB, 8), CB)
        lanes = slice(lane_group * 128, lane_group * 128 + 128)
        pltpu.store(dst.at[rows, lanes], src, mask=keep)

    def group(g, carry):
        base = g * GROUP
        xs_ref[...] = jnp.zeros(xs_ref.shape, f32)
        for m in range(GROUP):
            r = base + m + halo_rows
            for p in range(KP):
                w = wpos_ref[r * KP + p]
                slot = jnp.clip(w - NCD, 0, row_slots - 1)
                place(xs_ref, slot, m // 2, m % 2 == 1, r, p)
        xsb = xs_ref[...].astype(bf16)
        for k in range(local_k):
            s_ref[...] = jnp.zeros(s_ref.shape, f32)
            for m in range(GROUP):
                r = jloc_ref[(base + m) * local_k + k]
                for p in range(KP):
                    w = wpos_ref[r * KP + p]
                    slot = jnp.clip(w, 0, window_slots - 1)
                    place(s_ref, slot, m // 2, m % 2 == 1, r, p)
            parts = []
            for c in range(GROUP // 4):
                for mm in range(4):
                    t = tb_ref[base + 4 * c + mm].astype(f32)
                    if (k % 2 == 1) != (mm % 2 == 1):
                        t = pltpu.roll(t, B, 1)
                    keep = upper64 if mm % 2 == 1 else jnp.logical_not(upper64)
                    w_ref[mm * B:(mm + 1) * B, (mm // 2) * 128:(mm // 2) * 128 + 128] = jnp.where(
                        keep, t, 0.0
                    ).astype(bf16)
                window = s_ref[:, c * 256:(c + 1) * 256].astype(bf16)
                q = lax.dot_general(
                    window, w_ref[...], (((1,), (1,)), ((), ())), preferred_element_type=f32
                )
                parts.append(q.astype(bf16))
            qt = jnp.concatenate(parts, axis=1)
            gt_ref[...] += lax.dot_general(
                qt, xsb, (((1,), (1,)), ((), ())), preferred_element_type=f32
            )
        return carry

    lax.fori_loop(0, row_count // GROUP, group, 0)


def slab_terms_t(wpos, jloc, lower, own, upper, tb, halo_rows, row_count):
    local_k = tb.shape[2] // B
    window_width = 5 * NCD * CB
    row_width = 3 * NCD * CB
    kernel = functools.partial(slab_kernel, halo_rows, row_count, local_k)
    flops = 2 * row_count * local_k * (window_width * 256 * B + window_width * row_width * B)
    return pl.pallas_call(
        kernel,
        out_shape=jax.ShapeDtypeStruct((window_width, row_width), jnp.float32),
        in_specs=[
            pl.BlockSpec(memory_space=pltpu.SMEM),
            pl.BlockSpec(memory_space=pltpu.SMEM),
            pl.BlockSpec(memory_space=pl.ANY),
            pl.BlockSpec(memory_space=pl.ANY),
            pl.BlockSpec(memory_space=pl.ANY),
            pl.BlockSpec(memory_space=pltpu.VMEM),
        ],
        out_specs=pl.BlockSpec(memory_space=pltpu.VMEM),
        scratch_shapes=[
            pltpu.VMEM((row_count + 2 * halo_rows,) + own.shape[1:], own.dtype),
            pltpu.VMEM((window_width, GROUP * B), jnp.float32),
            pltpu.VMEM((row_width, GROUP * B), jnp.float32),
            pltpu.VMEM((256, 256), jnp.bfloat16),
            pltpu.SemaphoreType.DMA((3,)),
        ],
        compiler_params=pltpu.CompilerParams(vmem_limit_bytes=48 * 1024 * 1024),
        cost_estimate=pl.CostEstimate(
            flops=flops,
            bytes_accessed=(lower.size + own.size + upper.size) * 2 + tb.size * 2 + window_width * row_width * 4,
            transcendentals=0,
        ),
    )(wpos, jloc, lower, own, upper, tb)


def on_device(tangent_blocks, tangent_columns, prolong_blocks, prolong_columns):
    slab_count = lax.axis_size("blk")
    slab_index = lax.axis_index("blk")
    lane_count = lax.axis_size("lane")
    lane_index = lax.axis_index("lane")
    row_count = prolong_blocks.shape[0]
    halo_rows = row_count // 4
    coarse_width = NCD * CB
    fine_count = row_count * slab_count

    tail_rows, head_rows = send_rows(prolong_blocks, halo_rows)
    lower_blocks = shifted(tail_rows, "blk", 1)
    upper_blocks = shifted(head_rows, "blk", -1)
    lower_columns = shifted(prolong_columns[row_count - halo_rows:], "blk", 1)
    upper_columns = shifted(prolong_columns[:halo_rows], "blk", -1)
    near_columns = jnp.concatenate([lower_columns, prolong_columns, upper_columns], axis=0)
    wpos = ((near_columns // NCD - slab_index + 2) % slab_count) * NCD + near_columns % NCD
    wpos = wpos.astype(jnp.int32).reshape(-1)
    jloc = (tangent_columns - slab_index * row_count + halo_rows) % fine_count
    jloc = jnp.clip(jloc, 0, row_count + 2 * halo_rows - 1).astype(jnp.int32).reshape(-1)

    gt = slab_terms_t(wpos, jloc, lower_blocks, prolong_blocks, upper_blocks, tangent_blocks,
                      halo_rows, row_count)
    terms = gt.T.reshape(3, NCD, CB, 5 * coarse_width)

    shares = lax.dynamic_index_in_dim(terms, lane_index, axis=1, keepdims=False)
    for step in range(1, lane_count):
        piece = lax.dynamic_index_in_dim(
            terms, (lane_index + step) % lane_count, axis=1, keepdims=False
        )
        shares = shares + shifted(piece, "lane", step)
    from_lower = shifted(shares[2], "blk", 1)
    from_upper = shifted(shares[0], "blk", -1)
    coarse_band = (
        widen(shares[1], coarse_width, coarse_width)
        + widen(from_lower, 0, 2 * coarse_width)
        + widen(from_upper, 2 * coarse_width, 0)
    )
    return coarse_band[None]


def solution(mesh):
    return jax.shard_map(
        on_device,
        mesh=mesh,
        in_specs=(P("blk", None, "lane"), P("blk", "lane"), P("blk", None, None), P("blk", None)),
        out_specs=P(("blk", "lane"), None, None),
        check_vma=False,
    )
```

```python
import functools

import jax
import jax.numpy as jnp
from jax import lax
from jax.experimental import pallas as pl
from jax.experimental.pallas import tpu as pltpu
from jax.sharding import PartitionSpec as P

B = 64
CB = 24
KP = 8
NCD = 4
GROUP = 8


def shifted(value, axis, steps):
    count = lax.axis_size(axis)
    pairs = [(source, (source + steps) % count) for source in range(count)]
    return lax.ppermute(value, axis, pairs)


def widen(values, left_pad, right_pad):
    return jnp.pad(values, ((0, 0),) * (values.ndim - 1) + ((left_pad, right_pad),))


def slab_kernel(halo_rows, row_count, local_k, wpos_ref, jloc_ref, lower_ref, own_ref, upper_ref,
                tb_ref, gt_ref, pb_ref, s_ref, xs_ref, w_ref, sems):
    copies = [
        pltpu.make_async_copy(lower_ref.at[:, 0:CB], pb_ref.at[0:halo_rows], sems.at[0]),
        pltpu.make_async_copy(own_ref, pb_ref.at[halo_rows:halo_rows + row_count], sems.at[1]),
        pltpu.make_async_copy(
            upper_ref.at[:, 0:CB], pb_ref.at[halo_rows + row_count:2 * halo_rows + row_count],
            sems.at[2],
        ),
    ]
    for copy in copies:
        copy.start()
    window_slots = 5 * NCD
    row_slots = 3 * NCD
    f32 = jnp.float32
    bf16 = jnp.bfloat16
    upper24 = lax.broadcasted_iota(jnp.int32, (CB, 128), 1) >= B
    upper64 = lax.broadcasted_iota(jnp.int32, (B, 128), 1) >= B
    gt_ref[...] = jnp.zeros(gt_ref.shape, f32)
    w_ref[...] = jnp.zeros(w_ref.shape, bf16)
    for copy in copies:
        copy.wait()

    def place(dst, slot, lane_group, upper, r, p):
        src = pb_ref[r, :, (p // 2) * 128:(p // 2) * 128 + 128].astype(f32)
        if (p % 2 == 1) != upper:
            src = pltpu.roll(src, B, 1)
        keep = upper24 if upper else jnp.logical_not(upper24)
        rows = pl.ds(pl.multiple_of(slot * CB, 8), CB)
        lanes = slice(lane_group * 128, lane_group * 128 + 128)
        pltpu.store(dst.at[rows, lanes], src, mask=keep)

    def group(g, carry):
        base = g * GROUP
        xs_ref[...] = jnp.zeros(xs_ref.shape, f32)
        for m in range(GROUP):
            r = base + m + halo_rows
            for p in range(KP):
                w = wpos_ref[r * KP + p]
                slot = jnp.clip(w - NCD, 0, row_slots - 1)
                place(xs_ref, slot, m // 2, m % 2 == 1, r, p)
        xsb = xs_ref[...].astype(bf16)
        for k in range(local_k):
            s_ref[...] = jnp.zeros(s_ref.shape, f32)
            for m in range(GROUP):
                r = jloc_ref[(base + m) * local_k + k]
                for p in range(KP):
                    w = wpos_ref[r * KP + p]
                    slot = jnp.clip(w, 0, window_slots - 1)
                    place(s_ref, slot, m // 2, m % 2 == 1, r, p)
            parts = []
            for c in range(GROUP // 4):
                for mm in range(4):
                    t = tb_ref[base + 4 * c + mm].astype(f32)
                    if (k % 2 == 1) != (mm % 2 == 1):
                        t = pltpu.roll(t, B, 1)
                    keep = upper64 if mm % 2 == 1 else jnp.logical_not(upper64)
                    w_ref[mm * B:(mm + 1) * B, (mm // 2) * 128:(mm // 2) * 128 + 128] = jnp.where(
                        keep, t, 0.0
                    ).astype(bf16)
                window = s_ref[:, c * 256:(c + 1) * 256].astype(bf16)
                q = lax.dot_general(
                    window, w_ref[...], (((1,), (1,)), ((), ())), preferred_element_type=f32
                )
                parts.append(q.astype(bf16))
            qt = jnp.concatenate(parts, axis=1)
            gt_ref[...] += lax.dot_general(
                qt, xsb, (((1,), (1,)), ((), ())), preferred_element_type=f32
            )
        return carry

    lax.fori_loop(0, row_count // GROUP, group, 0)


def slab_terms_t(wpos, jloc, lower, own, upper, tb, halo_rows, row_count):
    local_k = tb.shape[2] // B
    window_width = 5 * NCD * CB
    row_width = 3 * NCD * CB
    kernel = functools.partial(slab_kernel, halo_rows, row_count, local_k)
    flops = 2 * row_count * local_k * (window_width * 256 * B + window_width * row_width * B)
    return pl.pallas_call(
        kernel,
        out_shape=jax.ShapeDtypeStruct((window_width, row_width), jnp.float32),
        in_specs=[
            pl.BlockSpec(memory_space=pltpu.SMEM),
            pl.BlockSpec(memory_space=pltpu.SMEM),
            pl.BlockSpec(memory_space=pl.ANY),
            pl.BlockSpec(memory_space=pl.ANY),
            pl.BlockSpec(memory_space=pl.ANY),
            pl.BlockSpec(memory_space=pltpu.VMEM),
        ],
        out_specs=pl.BlockSpec(memory_space=pltpu.VMEM),
        scratch_shapes=[
            pltpu.VMEM((row_count + 2 * halo_rows,) + own.shape[1:], own.dtype),
            pltpu.VMEM((window_width, GROUP * B), jnp.float32),
            pltpu.VMEM((row_width, GROUP * B), jnp.float32),
            pltpu.VMEM((256, 256), jnp.bfloat16),
            pltpu.SemaphoreType.DMA((3,)),
        ],
        compiler_params=pltpu.CompilerParams(vmem_limit_bytes=48 * 1024 * 1024),
        cost_estimate=pl.CostEstimate(
            flops=flops,
            bytes_accessed=(lower.size + own.size + upper.size) * 2 + tb.size * 2 + window_width * row_width * 4,
            transcendentals=0,
        ),
    )(wpos, jloc, lower, own, upper, tb)


def on_device(tangent_blocks, tangent_columns, prolong_blocks, prolong_columns):
    slab_count = lax.axis_size("blk")
    slab_index = lax.axis_index("blk")
    lane_count = lax.axis_size("lane")
    lane_index = lax.axis_index("lane")
    row_count = prolong_blocks.shape[0]
    halo_rows = row_count // 4
    coarse_width = NCD * CB
    fine_count = row_count * slab_count

    def with_columns(rows):
        blocks = prolong_blocks[rows]
        columns = prolong_columns[rows].astype(jnp.bfloat16)
        columns = jnp.pad(columns, ((0, 0), (0, blocks.shape[2] - KP)))[:, None, :]
        spare = jnp.zeros((blocks.shape[0], 32 - CB - 1, blocks.shape[2]), blocks.dtype)
        return jnp.concatenate([blocks, columns, spare], axis=1)

    lower_blocks = shifted(with_columns(slice(row_count - halo_rows, row_count)), "blk", 1)
    upper_blocks = shifted(with_columns(slice(0, halo_rows)), "blk", -1)
    lower_columns = lower_blocks[:, CB, :KP].astype(jnp.int32)
    upper_columns = upper_blocks[:, CB, :KP].astype(jnp.int32)
    near_columns = jnp.concatenate([lower_columns, prolong_columns, upper_columns], axis=0)
    wpos = ((near_columns // NCD - slab_index + 2) % slab_count) * NCD + near_columns % NCD
    wpos = wpos.astype(jnp.int32).reshape(-1)
    jloc = (tangent_columns - slab_index * row_count + halo_rows) % fine_count
    jloc = jnp.clip(jloc, 0, row_count + 2 * halo_rows - 1).astype(jnp.int32).reshape(-1)

    gt = slab_terms_t(wpos, jloc, lower_blocks, prolong_blocks, upper_blocks, tangent_blocks,
                      halo_rows, row_count)
    terms = gt.T.reshape(3, NCD, CB, 5 * coarse_width)

    shares = lax.dynamic_index_in_dim(terms, lane_index, axis=1, keepdims=False)
    for step in range(1, lane_count):
        piece = lax.dynamic_index_in_dim(
            terms, (lane_index + step) % lane_count, axis=1, keepdims=False
        )
        shares = shares + shifted(piece, "lane", step)
    from_lower = shifted(shares[2], "blk", 1)
    from_upper = shifted(shares[0], "blk", -1)
    coarse_band = (
        widen(shares[1], coarse_width, coarse_width)
        + widen(from_lower, 0, 2 * coarse_width)
        + widen(from_upper, 2 * coarse_width, 0)
    )
    return coarse_band[None]


def solution(mesh):
    return jax.shard_map(
        on_device,
        mesh=mesh,
        in_specs=(P("blk", None, "lane"), P("blk", "lane"), P("blk", None, None), P("blk", None)),
        out_specs=P(("blk", "lane"), None, None),
        check_vma=False,
    )
```

```python
import functools

import jax
import jax.numpy as jnp
from jax import lax
from jax.experimental import pallas as pl
from jax.experimental.pallas import tpu as pltpu
from jax.sharding import PartitionSpec as P

B = 64
CB = 24
KP = 8
NCD = 4
GROUP = 8


def shifted(value, axis, steps):
    count = lax.axis_size(axis)
    pairs = [(source, (source + steps) % count) for source in range(count)]
    return lax.ppermute(value, axis, pairs)


def widen(values, left_pad, right_pad):
    return jnp.pad(values, ((0, 0),) * (values.ndim - 1) + ((left_pad, right_pad),))


def slab_kernel(halo_rows, row_count, local_k, wpos_ref, jloc_ref, lower_ref, own_ref, upper_ref,
                tb_ref, gt_ref, pb_ref, s_ref, xs_ref, w_ref, sems):
    copies = [
        pltpu.make_async_copy(lower_ref, pb_ref.at[0:halo_rows], sems.at[0]),
        pltpu.make_async_copy(own_ref, pb_ref.at[halo_rows:halo_rows + row_count], sems.at[1]),
        pltpu.make_async_copy(
            upper_ref, pb_ref.at[halo_rows + row_count:2 * halo_rows + row_count], sems.at[2]
        ),
    ]
    for copy in copies:
        copy.start()
    window_slots = 5 * NCD
    row_slots = 3 * NCD
    f32 = jnp.float32
    bf16 = jnp.bfloat16
    upper24 = lax.broadcasted_iota(jnp.int32, (CB, 128), 1) >= B
    upper64 = lax.broadcasted_iota(jnp.int32, (B, 128), 1) >= B
    gt_ref[...] = jnp.zeros(gt_ref.shape, f32)
    w_ref[...] = jnp.zeros(w_ref.shape, bf16)
    for copy in copies:
        copy.wait()

    def place(dst, slot, lane_group, upper, r, p):
        src = pb_ref[r, :, (p // 2) * 128:(p // 2) * 128 + 128].astype(f32)
        if (p % 2 == 1) != upper:
            src = pltpu.roll(src, B, 1)
        keep = upper24 if upper else jnp.logical_not(upper24)
        rows = pl.ds(pl.multiple_of(slot * CB, 8), CB)
        lanes = slice(lane_group * 128, lane_group * 128 + 128)
        pltpu.store(dst.at[rows, lanes], src, mask=keep)

    def group(g, carry):
        base = g * GROUP
        xs_ref[...] = jnp.zeros(xs_ref.shape, f32)
        for m in range(GROUP):
            r = base + m + halo_rows
            for p in range(KP):
                w = wpos_ref[r * KP + p]
                slot = jnp.clip(w - NCD, 0, row_slots - 1)
                place(xs_ref, slot, m // 2, m % 2 == 1, r, p)
        xsb = xs_ref[...].astype(bf16)
        for k in range(local_k):
            s_ref[...] = jnp.zeros(s_ref.shape, f32)
            for m in range(GROUP):
                r = jloc_ref[(base + m) * local_k + k]
                for p in range(KP):
                    w = wpos_ref[r * KP + p]
                    slot = jnp.clip(w, 0, window_slots - 1)
                    place(s_ref, slot, m // 2, m % 2 == 1, r, p)
            parts = []
            for c in range(GROUP // 4):
                for mm in range(4):
                    t = tb_ref[base + 4 * c + mm].astype(f32)
                    if (k % 2 == 1) != (mm % 2 == 1):
                        t = pltpu.roll(t, B, 1)
                    keep = upper64 if mm % 2 == 1 else jnp.logical_not(upper64)
                    w_ref[mm * B:(mm + 1) * B, (mm // 2) * 128:(mm // 2) * 128 + 128] = jnp.where(
                        keep, t, 0.0
                    ).astype(bf16)
                window = s_ref[:, c * 256:(c + 1) * 256].astype(bf16)
                q = lax.dot_general(
                    window, w_ref[...], (((1,), (1,)), ((), ())), preferred_element_type=f32
                )
                parts.append(q.astype(bf16))
            qt = jnp.concatenate(parts, axis=1)
            gt_ref[...] += lax.dot_general(
                xsb, qt, (((1,), (1,)), ((), ())), preferred_element_type=f32
            )
        return carry

    lax.fori_loop(0, row_count // GROUP, group, 0)


def slab_terms_t(wpos, jloc, lower, own, upper, tb, halo_rows, row_count):
    local_k = tb.shape[2] // B
    window_width = 5 * NCD * CB
    row_width = 3 * NCD * CB
    kernel = functools.partial(slab_kernel, halo_rows, row_count, local_k)
    flops = 2 * row_count * local_k * (window_width * 256 * B + window_width * row_width * B)
    return pl.pallas_call(
        kernel,
        out_shape=jax.ShapeDtypeStruct((row_width, window_width), jnp.float32),
        in_specs=[
            pl.BlockSpec(memory_space=pltpu.SMEM),
            pl.BlockSpec(memory_space=pltpu.SMEM),
            pl.BlockSpec(memory_space=pl.ANY),
            pl.BlockSpec(memory_space=pl.ANY),
            pl.BlockSpec(memory_space=pl.ANY),
            pl.BlockSpec(memory_space=pltpu.VMEM),
        ],
        out_specs=pl.BlockSpec(memory_space=pltpu.VMEM),
        scratch_shapes=[
            pltpu.VMEM((row_count + 2 * halo_rows,) + own.shape[1:], own.dtype),
            pltpu.VMEM((window_width, GROUP * B), jnp.float32),
            pltpu.VMEM((row_width, GROUP * B), jnp.float32),
            pltpu.VMEM((256, 256), jnp.bfloat16),
            pltpu.SemaphoreType.DMA((3,)),
        ],
        compiler_params=pltpu.CompilerParams(vmem_limit_bytes=48 * 1024 * 1024),
        cost_estimate=pl.CostEstimate(
            flops=flops,
            bytes_accessed=(lower.size + own.size + upper.size) * 2 + tb.size * 2 + window_width * row_width * 4,
            transcendentals=0,
        ),
    )(wpos, jloc, lower, own, upper, tb)


def on_device(tangent_blocks, tangent_columns, prolong_blocks, prolong_columns):
    slab_count = lax.axis_size("blk")
    slab_index = lax.axis_index("blk")
    lane_count = lax.axis_size("lane")
    lane_index = lax.axis_index("lane")
    row_count = prolong_blocks.shape[0]
    halo_rows = row_count // 4
    coarse_width = NCD * CB
    fine_count = row_count * slab_count

    lower_blocks = shifted(prolong_blocks[row_count - halo_rows:], "blk", 1)
    upper_blocks = shifted(prolong_blocks[:halo_rows], "blk", -1)
    lower_columns = shifted(prolong_columns[row_count - halo_rows:], "blk", 1)
    upper_columns = shifted(prolong_columns[:halo_rows], "blk", -1)
    near_columns = jnp.concatenate([lower_columns, prolong_columns, upper_columns], axis=0)
    wpos = ((near_columns // NCD - slab_index + 2) % slab_count) * NCD + near_columns % NCD
    wpos = wpos.astype(jnp.int32).reshape(-1)
    jloc = (tangent_columns - slab_index * row_count + halo_rows) % fine_count
    jloc = jnp.clip(jloc, 0, row_count + 2 * halo_rows - 1).astype(jnp.int32).reshape(-1)

    gt = slab_terms_t(wpos, jloc, lower_blocks, prolong_blocks, upper_blocks, tangent_blocks,
                      halo_rows, row_count)
    terms = gt.reshape(3, NCD, CB, 5 * coarse_width)

    shares = lax.dynamic_index_in_dim(terms, lane_index, axis=1, keepdims=False)
    for step in range(1, lane_count):
        piece = lax.dynamic_index_in_dim(
            terms, (lane_index + step) % lane_count, axis=1, keepdims=False
        )
        shares = shares + shifted(piece, "lane", step)
    from_lower = shifted(shares[2], "blk", 1)
    from_upper = shifted(shares[0], "blk", -1)
    coarse_band = (
        widen(shares[1], coarse_width, coarse_width)
        + widen(from_lower, 0, 2 * coarse_width)
        + widen(from_upper, 2 * coarse_width, 0)
    )
    return coarse_band[None]


def solution(mesh):
    return jax.shard_map(
        on_device,
        mesh=mesh,
        in_specs=(P("blk", None, "lane"), P("blk", "lane"), P("blk", None, None), P("blk", None)),
        out_specs=P(("blk", "lane"), None, None),
        check_vma=False,
    )
```

```python
import functools

import jax
import jax.numpy as jnp
from jax import lax
from jax.experimental import pallas as pl
from jax.experimental.pallas import tpu as pltpu
from jax.sharding import PartitionSpec as P

B = 64
CB = 24
KP = 8
NCD = 4
GROUP = 16


def shifted(value, axis, steps):
    count = lax.axis_size(axis)
    pairs = [(source, (source + steps) % count) for source in range(count)]
    return lax.ppermute(value, axis, pairs)


def widen(values, left_pad, right_pad):
    return jnp.pad(values, ((0, 0),) * (values.ndim - 1) + ((left_pad, right_pad),))


def slab_kernel(halo_rows, row_count, local_k, wpos_ref, jloc_ref, lower_ref, own_ref, upper_ref,
                tb_ref, gt_ref, pb_ref, s_ref, xs_ref, w_ref, sems):
    copies = [
        pltpu.make_async_copy(lower_ref, pb_ref.at[0:halo_rows], sems.at[0]),
        pltpu.make_async_copy(own_ref, pb_ref.at[halo_rows:halo_rows + row_count], sems.at[1]),
        pltpu.make_async_copy(
            upper_ref, pb_ref.at[halo_rows + row_count:2 * halo_rows + row_count], sems.at[2]
        ),
    ]
    for copy in copies:
        copy.start()
    window_slots = 5 * NCD
    row_slots = 3 * NCD
    f32 = jnp.float32
    bf16 = jnp.bfloat16
    upper24 = lax.broadcasted_iota(jnp.int32, (CB, 128), 1) >= B
    upper64 = lax.broadcasted_iota(jnp.int32, (B, 128), 1) >= B
    gt_ref[...] = jnp.zeros(gt_ref.shape, f32)
    w_ref[...] = jnp.zeros(w_ref.shape, bf16)
    for copy in copies:
        copy.wait()

    def place(dst, slot, lane_group, upper, r, p):
        src = pb_ref[r, :, (p // 2) * 128:(p // 2) * 128 + 128].astype(f32)
        if (p % 2 == 1) != upper:
            src = pltpu.roll(src, B, 1)
        keep = upper24 if upper else jnp.logical_not(upper24)
        rows = pl.ds(pl.multiple_of(slot * CB, 8), CB)
        lanes = slice(lane_group * 128, lane_group * 128 + 128)
        pltpu.store(dst.at[rows, lanes], src, mask=keep)

    def group(g, carry):
        base = g * GROUP
        xs_ref[...] = jnp.zeros(xs_ref.shape, f32)
        for m in range(GROUP):
            r = base + m + halo_rows
            for p in range(KP):
                w = wpos_ref[r * KP + p]
                slot = jnp.clip(w - NCD, 0, row_slots - 1)
                place(xs_ref, slot, m // 2, m % 2 == 1, r, p)
        xsb = xs_ref[...].astype(bf16)
        for k in range(local_k):
            s_ref[...] = jnp.zeros(s_ref.shape, f32)
            for m in range(GROUP):
                r = jloc_ref[(base + m) * local_k + k]
                for p in range(KP):
                    w = wpos_ref[r * KP + p]
                    slot = jnp.clip(w, 0, window_slots - 1)
                    place(s_ref, slot, m // 2, m % 2 == 1, r, p)
            parts = []
            for c in range(GROUP // 4):
                for mm in range(4):
                    t = tb_ref[base + 4 * c + mm].astype(f32)
                    if (k % 2 == 1) != (mm % 2 == 1):
                        t = pltpu.roll(t, B, 1)
                    keep = upper64 if mm % 2 == 1 else jnp.logical_not(upper64)
                    w_ref[mm * B:(mm + 1) * B, (mm // 2) * 128:(mm // 2) * 128 + 128] = jnp.where(
                        keep, t, 0.0
                    ).astype(bf16)
                window = s_ref[:, c * 256:(c + 1) * 256].astype(bf16)
                q = lax.dot_general(
                    window, w_ref[...], (((1,), (1,)), ((), ())), preferred_element_type=f32
                )
                parts.append(q.astype(bf16))
            qt = jnp.concatenate(parts, axis=1)
            gt_ref[...] += lax.dot_general(
                xsb, qt, (((1,), (1,)), ((), ())), preferred_element_type=f32
            )
        return carry

    lax.fori_loop(0, row_count // GROUP, group, 0)


def slab_terms_t(wpos, jloc, lower, own, upper, tb, halo_rows, row_count):
    local_k = tb.shape[2] // B
    window_width = 5 * NCD * CB
    row_width = 3 * NCD * CB
    kernel = functools.partial(slab_kernel, halo_rows, row_count, local_k)
    flops = 2 * row_count * local_k * (window_width * 256 * B + window_width * row_width * B)
    return pl.pallas_call(
        kernel,
        out_shape=jax.ShapeDtypeStruct((row_width, window_width), jnp.float32),
        in_specs=[
            pl.BlockSpec(memory_space=pltpu.SMEM),
            pl.BlockSpec(memory_space=pltpu.SMEM),
            pl.BlockSpec(memory_space=pl.ANY),
            pl.BlockSpec(memory_space=pl.ANY),
            pl.BlockSpec(memory_space=pl.ANY),
            pl.BlockSpec(memory_space=pltpu.VMEM),
        ],
        out_specs=pl.BlockSpec(memory_space=pltpu.VMEM),
        scratch_shapes=[
            pltpu.VMEM((row_count + 2 * halo_rows,) + own.shape[1:], own.dtype),
            pltpu.VMEM((window_width, GROUP * B), jnp.float32),
            pltpu.VMEM((row_width, GROUP * B), jnp.float32),
            pltpu.VMEM((256, 256), jnp.bfloat16),
            pltpu.SemaphoreType.DMA((3,)),
        ],
        compiler_params=pltpu.CompilerParams(vmem_limit_bytes=48 * 1024 * 1024),
        cost_estimate=pl.CostEstimate(
            flops=flops,
            bytes_accessed=(lower.size + own.size + upper.size) * 2 + tb.size * 2 + window_width * row_width * 4,
            transcendentals=0,
        ),
    )(wpos, jloc, lower, own, upper, tb)


def on_device(tangent_blocks, tangent_columns, prolong_blocks, prolong_columns):
    slab_count = lax.axis_size("blk")
    slab_index = lax.axis_index("blk")
    lane_count = lax.axis_size("lane")
    lane_index = lax.axis_index("lane")
    row_count = prolong_blocks.shape[0]
    halo_rows = row_count // 4
    coarse_width = NCD * CB
    fine_count = row_count * slab_count

    lower_blocks = shifted(prolong_blocks[row_count - halo_rows:], "blk", 1)
    upper_blocks = shifted(prolong_blocks[:halo_rows], "blk", -1)
    lower_columns = shifted(prolong_columns[row_count - halo_rows:], "blk", 1)
    upper_columns = shifted(prolong_columns[:halo_rows], "blk", -1)
    near_columns = jnp.concatenate([lower_columns, prolong_columns, upper_columns], axis=0)
    wpos = ((near_columns // NCD - slab_index + 2) % slab_count) * NCD + near_columns % NCD
    wpos = wpos.astype(jnp.int32).reshape(-1)
    jloc = (tangent_columns - slab_index * row_count + halo_rows) % fine_count
    jloc = jnp.clip(jloc, 0, row_count + 2 * halo_rows - 1).astype(jnp.int32).reshape(-1)

    gt = slab_terms_t(wpos, jloc, lower_blocks, prolong_blocks, upper_blocks, tangent_blocks,
                      halo_rows, row_count)
    terms = gt.reshape(3, NCD, CB, 5 * coarse_width)

    shares = lax.dynamic_index_in_dim(terms, lane_index, axis=1, keepdims=False)
    for step in range(1, lane_count):
        piece = lax.dynamic_index_in_dim(
            terms, (lane_index + step) % lane_count, axis=1, keepdims=False
        )
        shares = shares + shifted(piece, "lane", step)
    from_lower = shifted(shares[2], "blk", 1)
    from_upper = shifted(shares[0], "blk", -1)
    coarse_band = (
        widen(shares[1], coarse_width, coarse_width)
        + widen(from_lower, 0, 2 * coarse_width)
        + widen(from_upper, 2 * coarse_width, 0)
    )
    return coarse_band[None]


def solution(mesh):
    return jax.shard_map(
        on_device,
        mesh=mesh,
        in_specs=(P("blk", None, "lane"), P("blk", "lane"), P("blk", None, None), P("blk", None)),
        out_specs=P(("blk", "lane"), None, None),
        check_vma=False,
    )
```

```python
import functools

import jax
import jax.numpy as jnp
from jax import lax
from jax.experimental import pallas as pl
from jax.experimental.pallas import tpu as pltpu
from jax.sharding import PartitionSpec as P

B = 64
CB = 24
KP = 8
NCD = 4
GROUP = 16


def shifted(value, axis, steps):
    count = lax.axis_size(axis)
    pairs = [(source, (source + steps) % count) for source in range(count)]
    return lax.ppermute(value, axis, pairs)


def widen(values, left_pad, right_pad):
    return jnp.pad(values, ((0, 0),) * (values.ndim - 1) + ((left_pad, right_pad),))


def slab_kernel(halo_rows, row_count, local_k, wpos_ref, jloc_ref, lower_ref, own_ref, upper_ref,
                tb_ref, gt_ref, pb_ref, s_ref, xs_ref, w_ref, sems):
    copies = [
        pltpu.make_async_copy(lower_ref, pb_ref.at[0:halo_rows], sems.at[0]),
        pltpu.make_async_copy(own_ref, pb_ref.at[halo_rows:halo_rows + row_count], sems.at[1]),
        pltpu.make_async_copy(
            upper_ref, pb_ref.at[halo_rows + row_count:2 * halo_rows + row_count], sems.at[2]
        ),
    ]
    for copy in copies:
        copy.start()
    window_slots = 5 * NCD
    row_slots = 3 * NCD
    f32 = jnp.float32
    bf16 = jnp.bfloat16
    upper24 = lax.broadcasted_iota(jnp.int32, (CB, 128), 1) >= B
    upper64 = lax.broadcasted_iota(jnp.int32, (B, 128), 1) >= B
    gt_ref[...] = jnp.zeros(gt_ref.shape, f32)
    w_ref[...] = jnp.zeros(w_ref.shape, bf16)
    for copy in copies:
        copy.wait()

    def place(dst, slot, lane_group, upper, r, p):
        src = pb_ref[r, :, (p // 2) * 128:(p // 2) * 128 + 128].astype(f32)
        if (p % 2 == 1) != upper:
            src = pltpu.roll(src, B, 1)
        keep = upper24 if upper else jnp.logical_not(upper24)
        rows = pl.ds(pl.multiple_of(slot * CB, 8), CB)
        lanes = slice(lane_group * 128, lane_group * 128 + 128)
        pltpu.store(dst.at[rows, lanes], src, mask=keep)

    def group(g, carry):
        base = g * GROUP
        xs_ref[...] = jnp.zeros(xs_ref.shape, f32)
        for m in range(GROUP):
            r = base + m + halo_rows
            for p in range(KP):
                w = wpos_ref[r * KP + p]
                slot = jnp.clip(w - NCD, 0, row_slots - 1)
                place(xs_ref, slot, m // 2, m % 2 == 1, r, p)
        xsb = xs_ref[...].astype(bf16)
        for k in range(local_k):
            s_ref[...] = jnp.zeros(s_ref.shape, f32)
            for m in range(GROUP):
                r = jloc_ref[(base + m) * local_k + k]
                for p in range(KP):
                    w = wpos_ref[r * KP + p]
                    slot = jnp.clip(w, 0, window_slots - 1)
                    place(s_ref, slot, m // 2, m % 2 == 1, r, p)
            parts = []
            for c in range(GROUP // 4):
                for mm in range(4):
                    t = tb_ref[base + 4 * c + mm].astype(f32)
                    if (k % 2 == 1) != (mm % 2 == 1):
                        t = pltpu.roll(t, B, 1)
                    keep = upper64 if mm % 2 == 1 else jnp.logical_not(upper64)
                    w_ref[mm * B:(mm + 1) * B, (mm // 2) * 128:(mm // 2) * 128 + 128] = jnp.where(
                        keep, t, 0.0
                    ).astype(bf16)
                window = s_ref[:, c * 256:(c + 1) * 256].astype(bf16)
                q = lax.dot_general(
                    window, w_ref[...], (((1,), (1,)), ((), ())), preferred_element_type=f32
                )
                parts.append(q.astype(bf16))
            qt = jnp.concatenate(parts, axis=1)
            gt_ref[...] += lax.dot_general(
                xsb, qt, (((1,), (1,)), ((), ())), preferred_element_type=f32
            )
        return carry

    lax.fori_loop(0, row_count // GROUP, group, 0)


def slab_terms_t(wpos, jloc, lower, own, upper, tb, halo_rows, row_count):
    local_k = tb.shape[2] // B
    window_width = 5 * NCD * CB
    row_width = 3 * NCD * CB
    kernel = functools.partial(slab_kernel, halo_rows, row_count, local_k)
    flops = 2 * row_count * local_k * (window_width * 256 * B + window_width * row_width * B)
    return pl.pallas_call(
        kernel,
        out_shape=jax.ShapeDtypeStruct((row_width, window_width), jnp.float32),
        in_specs=[
            pl.BlockSpec(memory_space=pltpu.SMEM),
            pl.BlockSpec(memory_space=pltpu.SMEM),
            pl.BlockSpec(memory_space=pl.ANY),
            pl.BlockSpec(memory_space=pl.ANY),
            pl.BlockSpec(memory_space=pl.ANY),
            pl.BlockSpec(memory_space=pltpu.VMEM),
        ],
        out_specs=pl.BlockSpec(memory_space=pltpu.VMEM),
        scratch_shapes=[
            pltpu.VMEM((row_count + 2 * halo_rows,) + own.shape[1:], own.dtype),
            pltpu.VMEM((window_width, GROUP * B), jnp.float32),
            pltpu.VMEM((row_width, GROUP * B), jnp.float32),
            pltpu.VMEM((256, 256), jnp.bfloat16),
            pltpu.SemaphoreType.DMA((3,)),
        ],
        compiler_params=pltpu.CompilerParams(vmem_limit_bytes=48 * 1024 * 1024),
        cost_estimate=pl.CostEstimate(
            flops=flops,
            bytes_accessed=(lower.size + own.size + upper.size) * 2 + tb.size * 2 + window_width * row_width * 4,
            transcendentals=0,
        ),
    )(wpos, jloc, lower, own, upper, tb)


def on_device(tangent_blocks, tangent_columns, prolong_blocks, prolong_columns):
    slab_count = lax.axis_size("blk")
    slab_index = lax.axis_index("blk")
    lane_count = lax.axis_size("lane")
    lane_index = lax.axis_index("lane")
    row_count = prolong_blocks.shape[0]
    halo_rows = row_count // 4
    coarse_width = NCD * CB
    fine_count = row_count * slab_count

    lower_blocks = shifted(prolong_blocks[row_count - halo_rows:], "blk", 1)
    upper_blocks = shifted(prolong_blocks[:halo_rows], "blk", -1)
    lower_columns = shifted(prolong_columns[row_count - halo_rows:], "blk", 1)
    upper_columns = shifted(prolong_columns[:halo_rows], "blk", -1)
    near_columns = jnp.concatenate([lower_columns, prolong_columns, upper_columns], axis=0)
    wpos = ((near_columns // NCD - slab_index + 2) % slab_count) * NCD + near_columns % NCD
    wpos = wpos.astype(jnp.int32).reshape(-1)
    jloc = (tangent_columns - slab_index * row_count + halo_rows) % fine_count
    jloc = jnp.clip(jloc, 0, row_count + 2 * halo_rows - 1).astype(jnp.int32).reshape(-1)

    gt = slab_terms_t(wpos, jloc, lower_blocks, prolong_blocks, upper_blocks, tangent_blocks,
                      halo_rows, row_count)
    terms = gt.reshape(3, NCD, CB, 5 * coarse_width)

    shares = lax.dynamic_index_in_dim(terms, lane_index, axis=1, keepdims=False)
    for step in sorted(range(1, lane_count), key=lambda s: min(s, lane_count - s)):
        piece = lax.dynamic_index_in_dim(
            terms, (lane_index + step) % lane_count, axis=1, keepdims=False
        )
        shares = shares + shifted(piece, "lane", step)
    from_lower = shifted(shares[2], "blk", 1)
    from_upper = shifted(shares[0], "blk", -1)
    coarse_band = (
        widen(shares[1], coarse_width, coarse_width)
        + widen(from_lower, 0, 2 * coarse_width)
        + widen(from_upper, 2 * coarse_width, 0)
    )
    return coarse_band[None]


def solution(mesh):
    return jax.shard_map(
        on_device,
        mesh=mesh,
        in_specs=(P("blk", None, "lane"), P("blk", "lane"), P("blk", None, None), P("blk", None)),
        out_specs=P(("blk", "lane"), None, None),
        check_vma=False,
    )
```
